512 devices in a mesh: phase: 8 (over y, core), ctx: 64 (over z, x).
Axes of the slice: x: 4, y: 4, z: 16, core: 2. Of those that a mesh axis runs over, the one named last changes fastest.
Arguments:
- mixer_input: bfloat16 [8, 8192, 4096], P('phase', 'ctx'), may hold values from -6 to 6
- state_proj: bfloat16 [8, 8192, 2048], P('phase', 'ctx'), may hold values from -6 to 6
- dt_raw: bfloat16 [8, 8192, 64], P('phase', 'ctx'), may hold values from -4 to 4
- decay_rate: float32 [8, 64], P('phase'), may hold values from 0.00048828125 to 0.05
- dt_bias: float32 [8, 64], P('phase'), may hold values from -1 to 1
- skip_gain: float32 [8, 64], P('phase'), may hold values from 0.5 to 1.5
- mamba_gain: float32 [8, 4096], P('phase'), may hold values from 0.5 to 1.5
- keys_values: bfloat16 [8, 8192, 512], P('phase', 'ctx'), may hold values from -160 to 160
- attn_gain: float32 [8, 4096], P('phase'), may hold values from 0.5 to 1.5
- documents: int32 [8, 8192], P('phase'), may hold values from 0 to 31, never falling along the last dimension, each value on 1 to 512 neighbouring positions
- placement_perm: int32 [64], replicated, may hold values from 0 to 63, each once
Outputs:
- handed: bfloat16 [8, 8192, 4096], P('phase', 'ctx')
The draws below stay inside these ranges and needn't reach their ends.
Inputs may be any that keep to these rules, and one draw needn't show every extreme that they name: Positions 128 placement_perm[d] to 128 placement_perm[d] + 127 lie at index d of ctx; every block once. Each phase's window holds 32 documents in order, each of 1 to 512 positions, one of exactly 512.
All inputs are finite; a program needn't handle non-finite values.
Results may differ from the reference program's by a relative error of at most 0.012.
Values may be sent and summed in bfloat16 or wider, within the bound.
No kernel may reach another device: no remote copies, remote signals or barrier semaphores. Data moves between devices by JAX's collectives and lax.ppermute only.
A program may use at most 128 MiB of HBM per device.

```python
import math
import jax
import jax.numpy as jnp
import numpy as np
from jax import lax

HEADS = 64
HEAD_DIM = 64
GROUPS = 8
STATE = 128
QHEADS = 32
KVHEADS = 2
QDIM = 128
TOK_DEV = 128
INNER = 4096
TOKENS = 8192
DOC_MOST = 512
DOCS = 32
N_PHASE = 8
N_CTX = 64


def draw_keys_values(key, part):
    first_key = jax.random.fold_in(key, 11)
    entries = jax.random.truncated_normal(first_key, -4.0, 4.0, (N_PHASE, TOKENS, 2, KVHEADS * QDIM), jnp.float32)
    return entries.reshape(N_PHASE, TOKENS, 2 * KVHEADS * QDIM).astype(jnp.bfloat16)


def levels(key, shape, pieces, smallest, top_value):
    loudness, own = 1.0, jax.random.fold_in(key, 6)
    for axis_at, shards_of in pieces:
        heights = jnp.exp(jax.random.uniform(jax.random.fold_in(own, axis_at), (shards_of,), jnp.float32, smallest / len(pieces), top_value / len(pieces)))
        loudness = loudness * jnp.repeat(heights, shape[axis_at] // shards_of).reshape([-1 if axis == axis_at else 1 for axis in range(len(shape))])
    return loudness


def split_up(count, total, reach, slope):
    loads = [(1 << 20) // math.isqrt(grade ** slope) + 1 for grade in range(2, count + 1)]
    surplus, counts = total - reach - (count - 1), [1] * (count - 1)
    while surplus > 0:
        movable = [i for i in range(count - 1) if counts[i] < reach]
        whole, left = sum([loads[i] for i in movable]), surplus
        for i in movable:
            more = min(reach - counts[i], max(1, left * loads[i] // whole), surplus)
            counts[i] = counts[i] + more
            surplus = surplus - more
    return np.array([reach] + counts)


def ragged_sizes(key, number_of, total, bound, slope):
    if number_of == 2:
        one = jax.random.randint(key, (), max(1, total - bound), min(bound, total - 1) + 1)
        return jnp.stack([one, total - one])
    sizes = jnp.asarray(split_up(number_of, total, bound, slope), jnp.int32)
    twos = (number_of - 1) // 2
    giver, taker = sizes[1:1 + 2 * twos:2], sizes[2:2 + 2 * twos:2]
    margin = jnp.minimum(giver - 1, bound - taker)
    shifted = jax.random.randint(jax.random.fold_in(key, 1), (twos,), 0, 1 << 20) % (margin + 1)
    sizes = sizes.at[1:1 + 2 * twos:2].set(giver - shifted).at[2:2 + 2 * twos:2].set(taker + shifted)
    return sizes[jax.random.permutation(jax.random.fold_in(key, 2), number_of)]


def centred(key, shape, width, reach, split=(), held_as=jnp.bfloat16):
    values = jax.random.normal(key, shape, jnp.float32) * width
    if len(split) > 0:
        values = levels(key, shape, split, -0.22, 0.18) * values
    return jnp.clip(values, min=-reach, max=reach).astype(held_as)


def setup_inputs(seed: int = 0) -> dict:
    splits = jax.random.split(jax.random.key(seed), 12)
    return {
        "mixer_input": centred(splits[0], (N_PHASE, TOKENS, INNER), 1.0, 6.0, ((0, 8), (1, 64))),
        "state_proj": centred(splits[1], (N_PHASE, TOKENS, GROUPS * 2 * STATE), 1.0, 6.0, ((0, 8), (1, 64))),
        "dt_raw": centred(splits[2], (N_PHASE, TOKENS, HEADS), 1.0, 4.0, ((0, 8), (1, 64))),
        "decay_rate": jnp.clip(jnp.exp(math.log(0.05) - 4.6288867 * jax.random.uniform(splits[3], (N_PHASE, HEADS), jnp.float32) ** levels(splits[3], (N_PHASE, HEADS), ((0, 8),), -0.2, 0.2)), 0.00048828125, 0.05),
        "dt_bias": jnp.clip(jax.random.uniform(splits[4], (N_PHASE, HEADS), jnp.float32, -1.0, 1.0) * levels(splits[4], (N_PHASE, HEADS), ((0, 8),), -0.4, 0.0), -1.0, 1.0),
        "skip_gain": jnp.clip(0.5 + 1.0 * jax.random.uniform(splits[5], (N_PHASE, HEADS), jnp.float32) ** levels(splits[5], (N_PHASE, HEADS), ((0, 8),), -0.2, 0.2), 0.5, 1.5),
        "mamba_gain": jnp.clip(1.0 + 0.1 * jax.random.normal(splits[6], (N_PHASE, INNER), jnp.float32), 0.5, 1.5),
        "keys_values": draw_keys_values(jax.random.fold_in(splits[11], 71), 0),
        "attn_gain": jnp.clip(1.0 + 0.1 * jax.random.normal(splits[8], (N_PHASE, INNER), jnp.float32), 0.5, 1.5),
        "documents": jax.vmap(lambda own: jnp.searchsorted(jnp.cumsum(ragged_sizes(own, DOCS, TOKENS, DOC_MOST, 1)), jnp.arange(TOKENS), side="right"))(jax.random.split(splits[9], N_PHASE)).reshape((N_PHASE, TOKENS)).astype(jnp.int32),
        "placement_perm": jax.random.permutation(splits[10], N_CTX).astype(jnp.int32),
    }


precise = lax.Precision.HIGHEST
epsilon = 1e-05

def reorder_blocks(array, indices):
    blocks = array.reshape((N_CTX, TOK_DEV) + array.shape[1:])
    return blocks[indices].reshape(array.shape)

def group_norm(values, gain):
    grouped = values.reshape(values.shape[0], GROUPS, -1)
    normed = grouped * lax.rsqrt(lax.optimization_barrier(jnp.mean(grouped * grouped, axis=-1, keepdims=True)) + epsilon)
    return normed.reshape(values.shape) * gain

def split_blocks(array):
    return array.reshape((TOKENS // TOK_DEV, TOK_DEV) + array.shape[1:])

def mamba_mixer(values, projections, raw_steps, decay_rate, dt_bias, skip_gain, segment):
    within = HEADS // GROUPS
    step_sizes = jax.nn.softplus(raw_steps + dt_bias)
    log_decay = -decay_rate * step_sizes
    paired = projections.reshape(TOKENS, GROUPS, 2, STATE)
    inject = jnp.repeat(paired[:, :, 0], within, axis=1)
    readout = jnp.repeat(paired[:, :, 1], within, axis=1)
    scaled = values * step_sizes[:, :, None]
    block_seg = segment.reshape(TOKENS // TOK_DEV, TOK_DEV)
    seg_prev = jnp.concatenate([jnp.full((1,), -1, jnp.int32), block_seg[:-1, -1]])
    positions = jnp.arange(TOK_DEV)
    lower = positions[:, None] >= positions[None, :]

    def advance(carried, element):
        scaled_b, inject_b, readout_b, log_b, seg_b, prev_b = element
        cum_log = jnp.cumsum(log_b, axis=0)
        spread = cum_log[:, None, :] - cum_log[None, :, :]
        allowed = lower & (seg_b[:, None] == seg_b[None, :])
        decays = jnp.where(allowed[:, :, None], jnp.exp(jnp.minimum(spread, 0.0)), 0.0)
        scores = jnp.einsum('ihs,jhs->ijh', readout_b, inject_b, precision=precise)
        local_out = jnp.einsum('ijh,jhp->ihp', decays * scores, scaled_b, precision=precise)
        reach_mask = jnp.where((seg_b == prev_b)[:, None], jnp.exp(cum_log), 0.0)
        read_out = jnp.einsum('ihs,hps->ihp', readout_b, carried, precision=precise)
        ending = cum_log[-1]
        last_seg = seg_b[-1]
        to_end = jnp.where((seg_b == last_seg)[:, None], jnp.exp(ending[None, :] - cum_log), 0.0)
        fresh = jnp.einsum('jhp,jhs->hps', scaled_b * to_end[:, :, None], inject_b, precision=precise)
        kept = jnp.where(last_seg == prev_b, jnp.exp(ending)[:, None, None] * carried, 0.0)
        return (kept + fresh, local_out + read_out * reach_mask[:, :, None])
    initial = jnp.zeros((HEADS, HEAD_DIM, STATE), jnp.float32)
    elements = (split_blocks(scaled), split_blocks(inject), split_blocks(readout), split_blocks(log_decay), block_seg, seg_prev)
    outputs = lax.scan(advance, initial, elements)[1]
    return outputs.reshape(TOKENS, HEADS, HEAD_DIM) + skip_gain[:, None] * values

def attention(queries, keys, values, segment):
    repeat = QHEADS // KVHEADS
    query_rows = math.gcd(512, TOKENS)
    key_width = min(DOC_MOST + query_rows, TOKENS)
    score_scale = 1.0 / math.sqrt(QDIM)

    def one_block(first_row):
        key_start = jnp.maximum(first_row + query_rows - key_width, 0)
        q_block = lax.dynamic_slice_in_dim(queries, first_row, query_rows, 0).astype(jnp.float32)
        q_block = q_block.reshape(query_rows, KVHEADS, repeat, QDIM)
        k_block = lax.dynamic_slice_in_dim(keys, key_start, key_width, 0).astype(jnp.float32)
        v_block = lax.dynamic_slice_in_dim(values, key_start, key_width, 0).astype(jnp.float32)
        query_pos = first_row + jnp.arange(query_rows, dtype=jnp.int32)
        key_pos = key_start + jnp.arange(key_width, dtype=jnp.int32)
        query_seg = lax.dynamic_slice_in_dim(segment, first_row, query_rows, 0)
        key_seg = lax.dynamic_slice_in_dim(segment, key_start, key_width, 0)
        allowed = (query_seg[:, None] == key_seg[None, :]) & (key_pos[None, :] <= query_pos[:, None])
        logits = jnp.einsum('tgrd,kgd->grtk', q_block, k_block, precision=precise) * score_scale
        logits = jnp.where(allowed, logits, -1e+30)
        best_score = lax.optimization_barrier(jnp.max(logits, axis=-1, keepdims=True))
        weights = jnp.where(allowed, jnp.exp(logits - best_score), 0.0)
        total_weight = lax.optimization_barrier(jnp.sum(weights, axis=-1))
        rounded = lax.optimization_barrier(weights.astype(jnp.bfloat16)).astype(jnp.float32)
        blended = jnp.einsum('grtk,kgd->grtd', rounded, v_block, precision=precise) / total_weight[..., None]
        return blended.transpose(2, 0, 1, 3).reshape(query_rows, QHEADS * QDIM)
    starts = jnp.arange(0, TOKENS, query_rows, dtype=jnp.int32)
    return lax.map(one_block, starts).reshape(TOKENS, QHEADS * QDIM)

def section(mixer_input, state_proj, dt_raw, decay_rate, dt_bias, skip_gain, mamba_gain, keys_values, attn_gain, documents, placement_perm):
    inverse = jnp.zeros((N_CTX,), jnp.int32).at[placement_perm].set(jnp.arange(N_CTX, dtype=jnp.int32))
    seq_input = reorder_blocks(mixer_input, inverse).astype(jnp.float32)
    values = seq_input.reshape(TOKENS, HEADS, HEAD_DIM)
    projections = reorder_blocks(state_proj, inverse).astype(jnp.float32)
    raw_steps = reorder_blocks(dt_raw, inverse).astype(jnp.float32)
    mamba_out = mamba_mixer(values, projections, raw_steps, decay_rate, dt_bias, skip_gain, documents)
    mamba_out = mamba_out.reshape(TOKENS, HEADS * HEAD_DIM).astype(jnp.bfloat16)
    hidden = (seq_input + group_norm(mamba_out.astype(jnp.float32), mamba_gain)).astype(jnp.bfloat16)
    pairs = reorder_blocks(keys_values, inverse).reshape(TOKENS, 2, KVHEADS, QDIM)
    attended = attention(hidden.reshape(TOKENS, QHEADS, QDIM), pairs[:, 0], pairs[:, 1], documents)
    normed = attended * lax.rsqrt(lax.optimization_barrier(jnp.mean(attended * attended, axis=-1, keepdims=True)) + epsilon) * attn_gain
    result = (hidden.astype(jnp.float32) + normed).astype(jnp.bfloat16)
    return reorder_blocks(result, placement_perm)

def reference(mixer_input, state_proj, dt_raw, decay_rate, dt_bias, skip_gain, mamba_gain, keys_values, attn_gain, documents, placement_perm):

    def one_phase(arrays):
        return section(*arrays, placement_perm)
    results = lax.map(one_phase, (mixer_input, state_proj, dt_raw, decay_rate, dt_bias, skip_gain, mamba_gain, keys_values, attn_gain, documents))
    return jnp.roll(results, 1, axis=0)
```

```python
import math

import jax
import jax.numpy as jnp
from jax import lax
from jax.sharding import PartitionSpec as P

HEADS = 64
HEAD_DIM = 64
GROUPS = 8
STATE = 128
QHEADS = 32
KVHEADS = 2
QDIM = 128
HALO = 4


precise = lax.Precision.HIGHEST
epsilon = 1e-05


def passed_along(value, axis, steps):
    count = lax.axis_size(axis)
    pairs = [(source, (source + steps) % count) for source in range(count)]
    return lax.ppermute(value, axis, pairs)


def group_norm(values, gain):
    grouped = values.reshape(values.shape[0], GROUPS, -1)
    normed = grouped * lax.rsqrt(jnp.mean(grouped * grouped, axis=-1, keepdims=True) + epsilon)
    return normed.reshape(values.shape) * gain


def block_terms(values, inject, readout, step_sizes, rates, seg):
    length = values.shape[0]
    within = HEADS // GROUPS
    cum_log = jnp.cumsum(-rates * step_sizes, axis=0)
    positions = jnp.arange(length)
    allowed = (positions[:, None] >= positions[None, :]) & (seg[:, None] == seg[None, :])
    spread = cum_log.T[:, :, None] - cum_log.T[:, None, :]
    decays = jnp.where(allowed[None], jnp.exp(jnp.minimum(spread, 0.0)), 0.0)
    scores = jnp.einsum("tgs,ugs->gtu", readout, inject, preferred_element_type=jnp.float32)
    weights = decays.reshape(GROUPS, within, length, length) * scores[:, None]
    scaled = values * step_sizes[..., None]
    local_out = jnp.einsum(
        "gktu,ugkp->tgkp",
        weights,
        scaled.reshape(length, GROUPS, within, HEAD_DIM),
        precision=precise,
    ).reshape(values.shape)
    ending = cum_log[-1]
    to_end = jnp.where((seg == seg[-1])[:, None], jnp.exp(ending[None, :] - cum_log), 0.0)
    weighted = (scaled * to_end[..., None]).reshape(length, GROUPS, within, HEAD_DIM)
    states = jnp.einsum(
        "tgkp,tgs->gkps", weighted, inject.astype(jnp.float32), precision=precise
    ).reshape(HEADS, HEAD_DIM, STATE)
    return local_out, states, cum_log, ending


def on_device(
    mixer_input,
    state_proj,
    dt_raw,
    decay_rate,
    dt_bias,
    skip_gain,
    mamba_gain,
    keys_values,
    attn_gain,
    documents,
    placement_perm,
):
    devices = lax.axis_size("ctx")
    myself = lax.axis_index("ctx")
    tok_rows = mixer_input.shape[1]
    kv_cols = keys_values.shape[2]
    slice_cols = kv_cols // devices
    inverse = (
        jnp.zeros((devices,), jnp.int32)
        .at[placement_perm]
        .set(jnp.arange(devices, dtype=jnp.int32))
    )
    segment = documents[0]
    block_seg = segment.reshape(devices, tok_rows)
    seg_end = block_seg[:, -1]
    seg_prev = jnp.concatenate([jnp.full((1,), -1, jnp.int32), seg_end[:-1]])
    my_block = placement_perm[myself]
    my_seg = lax.dynamic_slice_in_dim(segment, my_block * tok_rows, tok_rows, 0)
    my_prev = seg_prev[my_block]

    inputs = mixer_input[0]
    values = inputs.astype(jnp.float32).reshape(tok_rows, HEADS, HEAD_DIM)
    paired = state_proj[0].reshape(tok_rows, GROUPS, 2, STATE)
    inject = paired[:, :, 0]
    readout = paired[:, :, 1]
    step_sizes = jax.nn.softplus(dt_raw[0].astype(jnp.float32) + dt_bias[0])
    local_out, states, cum_log, ending = block_terms(
        values, inject, readout, step_sizes, decay_rate[0], my_seg
    )

    kv = keys_values[0]
    kv_slices = kv.reshape(tok_rows, devices, slice_cols).transpose(1, 0, 2)
    kv_slices = kv_slices.reshape(devices, tok_rows * slice_cols)
    state_slots = states.astype(jnp.bfloat16).reshape(HEADS, HEAD_DIM * STATE)
    first = jnp.concatenate([state_slots, kv_slices], axis=1)
    got = lax.all_to_all(first, "ctx", split_axis=0, concat_axis=0, tiled=True)
    all_endings = lax.all_gather(ending, "ctx", axis=0, tiled=False)
    got_states = got[:, : HEAD_DIM * STATE].astype(jnp.float32)
    got_kv = got[:, HEAD_DIM * STATE :]

    ending_pos = all_endings[inverse, myself]
    running = jnp.cumsum(ending_pos)
    before = running - ending_pos
    positions = jnp.arange(devices)
    linked = (positions[None, :] < positions[:, None]) & (seg_end[None, :] == seg_prev[:, None])
    factors = jnp.where(
        linked, jnp.exp(jnp.minimum(before[:, None] - running[None, :], 0.0)), 0.0
    )
    by_device = factors[placement_perm][:, placement_perm]
    entering = jnp.dot(by_device, got_states, precision=precise)

    halo_blocks = placement_perm[:, None] - HALO + jnp.arange(HALO)[None, :]
    halo_src = inverse[jnp.clip(halo_blocks, 0, devices - 1)]
    halo = got_kv[halo_src].reshape(devices, HALO * tok_rows * slice_cols)
    second = jnp.concatenate([entering.astype(jnp.bfloat16), halo], axis=1)
    back = lax.all_to_all(second, "ctx", split_axis=0, concat_axis=0, tiled=True)
    enter_here = back[:, : HEAD_DIM * STATE].reshape(GROUPS, HEADS // GROUPS, HEAD_DIM, STATE)
    halo_here = back[:, HEAD_DIM * STATE :].reshape(devices, HALO * tok_rows, slice_cols)
    halo_kv = halo_here.transpose(1, 0, 2).reshape(HALO * tok_rows, kv_cols)

    reach = jnp.where((my_seg == my_prev)[:, None], jnp.exp(cum_log), 0.0)
    read_out = jnp.einsum(
        "tgs,gkps->tgkp", readout, enter_here, preferred_element_type=jnp.float32
    ).reshape(tok_rows, HEADS, HEAD_DIM)
    outputs = local_out + read_out * reach[..., None] + skip_gain[0][:, None] * values
    mamba_out = outputs.astype(jnp.bfloat16).reshape(tok_rows, HEADS * HEAD_DIM)
    residual = inputs.astype(jnp.float32) + group_norm(mamba_out.astype(jnp.float32), mamba_gain[0])
    hidden = residual.astype(jnp.bfloat16)

    repeat = QHEADS // KVHEADS
    queries = hidden.reshape(tok_rows, KVHEADS, repeat, QDIM)
    all_kv = jnp.concatenate([halo_kv, kv], axis=0).reshape(-1, 2, KVHEADS, QDIM)
    keys = all_kv[:, 0]
    vals = all_kv[:, 1]
    query_pos = my_block * tok_rows + jnp.arange(tok_rows, dtype=jnp.int32)
    key_pos = (my_block - HALO) * tok_rows + jnp.arange((HALO + 1) * tok_rows, dtype=jnp.int32)
    key_seg = jnp.take(segment, jnp.maximum(key_pos, 0))
    allowed = (
        (my_seg[:, None] == key_seg[None, :])
        & (key_pos[None, :] <= query_pos[:, None])
        & (key_pos[None, :] >= 0)
    )
    score_scale = 1.0 / math.sqrt(QDIM)
    logits = (
        jnp.einsum("tgrd,kgd->grtk", queries, keys, preferred_element_type=jnp.float32)
        * score_scale
    )
    logits = jnp.where(allowed, logits, -1e30)
    best = jnp.max(logits, axis=-1, keepdims=True)
    weights = jnp.where(allowed, jnp.exp(logits - best), 0.0)
    total_weight = jnp.sum(weights, axis=-1)
    blended = jnp.einsum(
        "grtk,kgd->grtd", weights.astype(jnp.bfloat16), vals, preferred_element_type=jnp.float32
    )
    attended = (
        (blended / total_weight[..., None]).transpose(2, 0, 1, 3).reshape(tok_rows, QHEADS * QDIM)
    )
    normed = (
        attended
        * lax.rsqrt(jnp.mean(attended * attended, axis=-1, keepdims=True) + epsilon)
        * attn_gain[0]
    )
    result = (hidden.astype(jnp.float32) + normed).astype(jnp.bfloat16)
    return passed_along(result[None], "phase", 1)


def solution(mesh):
    in_specs = (
        P("phase", "ctx", None),
        P("phase", "ctx", None),
        P("phase", "ctx", None),
        P("phase", None),
        P("phase", None),
        P("phase", None),
        P("phase", None),
        P("phase", "ctx", None),
        P("phase", None),
        P("phase", None),
        P(),
    )
    out_specs = P("phase", "ctx", None)
    return jax.shard_map(
        on_device, mesh=mesh, in_specs=in_specs, out_specs=out_specs, check_vma=False
    )
```

```python
import math

import jax
import jax.numpy as jnp
from jax import lax
from jax.sharding import PartitionSpec as P

HEADS = 64
HEAD_DIM = 64
GROUPS = 8
STATE = 128
QHEADS = 32
KVHEADS = 2
QDIM = 128
HALO = 4


precise = lax.Precision.HIGHEST
epsilon = 1e-05


def passed_along(value, axis, steps):
    count = lax.axis_size(axis)
    pairs = [(source, (source + steps) % count) for source in range(count)]
    return lax.ppermute(value, axis, pairs)


def group_norm(values, gain):
    grouped = values.reshape(values.shape[0], GROUPS, -1)
    normed = grouped * lax.rsqrt(jnp.mean(grouped * grouped, axis=-1, keepdims=True) + epsilon)
    return normed.reshape(values.shape) * gain


def block_terms(values, inject, readout, step_sizes, rates, seg):
    length = values.shape[0]
    within = HEADS // GROUPS
    cum_log = jnp.cumsum(-rates * step_sizes, axis=0)
    positions = jnp.arange(length)
    allowed = (positions[:, None] >= positions[None, :]) & (seg[:, None] == seg[None, :])
    spread = cum_log.T[:, :, None] - cum_log.T[:, None, :]
    decays = jnp.where(allowed[None], jnp.exp(jnp.minimum(spread, 0.0)), 0.0)
    scores = jnp.einsum("tgs,ugs->gtu", readout, inject, preferred_element_type=jnp.float32)
    weights = decays.reshape(GROUPS, within, length, length) * scores[:, None]
    scaled = values * step_sizes[..., None]
    local_out = jnp.einsum(
        "gktu,ugkp->tgkp",
        weights,
        scaled.reshape(length, GROUPS, within, HEAD_DIM),
        precision=precise,
    ).reshape(values.shape)
    ending = cum_log[-1]
    to_end = jnp.where((seg == seg[-1])[:, None], jnp.exp(ending[None, :] - cum_log), 0.0)
    weighted = (scaled * to_end[..., None]).reshape(length, GROUPS, within, HEAD_DIM)
    states = jnp.einsum(
        "tgkp,tgs->gkps", weighted, inject.astype(jnp.float32), precision=precise
    ).reshape(HEADS, HEAD_DIM, STATE)
    return local_out, states, cum_log, ending


def on_device(
    mixer_input,
    state_proj,
    dt_raw,
    decay_rate,
    dt_bias,
    skip_gain,
    mamba_gain,
    keys_values,
    attn_gain,
    documents,
    placement_perm,
):
    devices = lax.axis_size("ctx")
    myself = lax.axis_index("ctx")
    tok_rows = mixer_input.shape[1]
    kv_cols = keys_values.shape[2]
    slice_cols = kv_cols // devices
    inverse = (
        jnp.zeros((devices,), jnp.int32)
        .at[placement_perm]
        .set(jnp.arange(devices, dtype=jnp.int32))
    )
    segment = documents[0]
    block_seg = segment.reshape(devices, tok_rows)
    seg_end = block_seg[:, -1]
    seg_prev = jnp.concatenate([jnp.full((1,), -1, jnp.int32), seg_end[:-1]])
    my_block = placement_perm[myself]
    my_seg = lax.dynamic_slice_in_dim(segment, my_block * tok_rows, tok_rows, 0)
    my_prev = seg_prev[my_block]

    inputs = mixer_input[0]
    values = inputs.astype(jnp.float32).reshape(tok_rows, HEADS, HEAD_DIM)
    paired = state_proj[0].reshape(tok_rows, GROUPS, 2, STATE)
    inject = paired[:, :, 0]
    readout = paired[:, :, 1]
    step_sizes = jax.nn.softplus(dt_raw[0].astype(jnp.float32) + dt_bias[0])
    local_out, states, cum_log, ending = block_terms(
        values, inject, readout, step_sizes, decay_rate[0], my_seg
    )

    kv = keys_values[0]
    lanes = 128
    kv_rows = tok_rows * slice_cols // lanes
    kv_slices = kv.reshape(tok_rows, devices, slice_cols).transpose(1, 0, 2)
    kv_slices = kv_slices.reshape(devices, kv_rows, lanes)
    raw_cols = dt_raw[0].T.reshape(HEADS, 1, tok_rows)
    state_slots = states.astype(jnp.bfloat16)
    used = HEAD_DIM + kv_rows + 1
    padding = jnp.zeros((devices, -used % 8, lanes), jnp.bfloat16)
    first = jnp.concatenate([state_slots, kv_slices, raw_cols, padding], axis=1)
    got = lax.all_to_all(first, "ctx", split_axis=0, concat_axis=0, tiled=True)
    got_states = got[:, :HEAD_DIM].astype(jnp.float32)
    got_kv = got[:, HEAD_DIM : HEAD_DIM + kv_rows]
    got_raw = got[:, HEAD_DIM + kv_rows].astype(jnp.float32)

    my_rate = decay_rate[0][myself]
    my_bias = dt_bias[0][myself]
    my_steps = jax.nn.softplus(got_raw + my_bias)
    endings = jnp.cumsum(-my_rate * my_steps, axis=1)[:, -1]
    ending_pos = endings[inverse]
    running = jnp.cumsum(ending_pos)
    before = running - ending_pos
    positions = jnp.arange(devices)
    linked = (positions[None, :] < positions[:, None]) & (seg_end[None, :] == seg_prev[:, None])
    factors = jnp.where(
        linked, jnp.exp(jnp.minimum(before[:, None] - running[None, :], 0.0)), 0.0
    )
    by_device = factors[placement_perm][:, placement_perm]
    entering = jnp.einsum("ds,spn->dpn", by_device, got_states, precision=precise)

    halo_blocks = placement_perm[:, None] - HALO + jnp.arange(HALO)[None, :]
    halo_src = inverse[jnp.clip(halo_blocks, 0, devices - 1)]
    halo = got_kv[halo_src].reshape(devices, HALO * kv_rows, lanes)
    second = jnp.concatenate([entering.astype(jnp.bfloat16), halo], axis=1)
    back = lax.all_to_all(second, "ctx", split_axis=0, concat_axis=0, tiled=True)
    enter_here = back[:, :HEAD_DIM].reshape(GROUPS, HEADS // GROUPS, HEAD_DIM, STATE)
    halo_here = back[:, HEAD_DIM:].reshape(devices, HALO * tok_rows, slice_cols)
    halo_kv = halo_here.transpose(1, 0, 2).reshape(HALO * tok_rows, kv_cols)

    reach = jnp.where((my_seg == my_prev)[:, None], jnp.exp(cum_log), 0.0)
    read_out = jnp.einsum(
        "tgs,gkps->tgkp", readout, enter_here, preferred_element_type=jnp.float32
    ).reshape(tok_rows, HEADS, HEAD_DIM)
    outputs = local_out + read_out * reach[..., None] + skip_gain[0][:, None] * values
    mamba_out = outputs.astype(jnp.bfloat16).reshape(tok_rows, HEADS * HEAD_DIM)
    residual = inputs.astype(jnp.float32) + group_norm(mamba_out.astype(jnp.float32), mamba_gain[0])
    hidden = residual.astype(jnp.bfloat16)

    repeat = QHEADS // KVHEADS
    queries = hidden.reshape(tok_rows, KVHEADS, repeat, QDIM)
    all_kv = jnp.concatenate([halo_kv, kv], axis=0).reshape(-1, 2, KVHEADS, QDIM)
    keys = all_kv[:, 0]
    vals = all_kv[:, 1]
    query_pos = my_block * tok_rows + jnp.arange(tok_rows, dtype=jnp.int32)
    key_pos = (my_block - HALO) * tok_rows + jnp.arange((HALO + 1) * tok_rows, dtype=jnp.int32)
    key_seg = jnp.take(segment, jnp.maximum(key_pos, 0))
    allowed = (
        (my_seg[:, None] == key_seg[None, :])
        & (key_pos[None, :] <= query_pos[:, None])
        & (key_pos[None, :] >= 0)
    )
    score_scale = 1.0 / math.sqrt(QDIM)
    logits = (
        jnp.einsum("tgrd,kgd->grtk", queries, keys, preferred_element_type=jnp.float32)
        * score_scale
    )
    logits = jnp.where(allowed, logits, -1e30)
    best = jnp.max(logits, axis=-1, keepdims=True)
    weights = jnp.where(allowed, jnp.exp(logits - best), 0.0)
    total_weight = jnp.sum(weights, axis=-1)
    blended = jnp.einsum(
        "grtk,kgd->grtd", weights.astype(jnp.bfloat16), vals, preferred_element_type=jnp.float32
    )
    attended = (
        (blended / total_weight[..., None]).transpose(2, 0, 1, 3).reshape(tok_rows, QHEADS * QDIM)
    )
    normed = (
        attended
        * lax.rsqrt(jnp.mean(attended * attended, axis=-1, keepdims=True) + epsilon)
        * attn_gain[0]
    )
    result = (hidden.astype(jnp.float32) + normed).astype(jnp.bfloat16)
    return passed_along(result[None], "phase", 1)


def solution(mesh):
    in_specs = (
        P("phase", "ctx", None),
        P("phase", "ctx", None),
        P("phase", "ctx", None),
        P("phase", None),
        P("phase", None),
        P("phase", None),
        P("phase", None),
        P("phase", "ctx", None),
        P("phase", None),
        P("phase", None),
        P(),
    )
    out_specs = P("phase", "ctx", None)
    return jax.shard_map(
        on_device, mesh=mesh, in_specs=in_specs, out_specs=out_specs, check_vma=False
    )
```

```python
import math

import jax
import jax.numpy as jnp
from jax import lax
from jax.sharding import PartitionSpec as P

HEADS = 64
HEAD_DIM = 64
GROUPS = 8
STATE = 128
QHEADS = 32
KVHEADS = 2
QDIM = 128
HALO = 4
LANES = 128


precise = lax.Precision.HIGHEST
epsilon = 1e-05


def passed_along(value, axis, steps):
    count = lax.axis_size(axis)
    pairs = [(source, (source + steps) % count) for source in range(count)]
    return lax.ppermute(value, axis, pairs)


def group_norm(values, gain):
    grouped = values.reshape(values.shape[0], -1, HEADS // GROUPS * HEAD_DIM)
    normed = grouped * lax.rsqrt(jnp.mean(grouped * grouped, axis=-1, keepdims=True) + epsilon)
    return normed.reshape(values.shape) * gain


def block_terms(values, inject, readout, step_sizes, rates, seg):
    length, heads_here = values.shape[0], values.shape[1]
    groups_here = inject.shape[1]
    within = heads_here // groups_here
    cum_log = jnp.cumsum(-rates * step_sizes, axis=0)
    positions = jnp.arange(length)
    allowed = (positions[:, None] >= positions[None, :]) & (seg[:, None] == seg[None, :])
    spread = cum_log.T[:, :, None] - cum_log.T[:, None, :]
    decays = jnp.where(allowed[None], jnp.exp(jnp.minimum(spread, 0.0)), 0.0)
    scores = jnp.einsum("tgs,ugs->gtu", readout, inject, preferred_element_type=jnp.float32)
    weights = decays.reshape(groups_here, within, length, length) * scores[:, None]
    scaled = values * step_sizes[..., None]
    local_out = jnp.einsum(
        "gktu,ugkp->tgkp",
        weights,
        scaled.reshape(length, groups_here, within, HEAD_DIM),
        precision=precise,
    ).reshape(values.shape)
    ending = cum_log[-1]
    to_end = jnp.where((seg == seg[-1])[:, None], jnp.exp(ending[None, :] - cum_log), 0.0)
    weighted = (scaled * to_end[..., None]).reshape(length, groups_here, within, HEAD_DIM)
    states = jnp.einsum(
        "tgkp,tgs->gkps", weighted, inject.astype(jnp.float32), precision=precise
    ).reshape(heads_here, HEAD_DIM, STATE)
    return local_out, states, cum_log


def on_device(
    mixer_input,
    state_proj,
    dt_raw,
    decay_rate,
    dt_bias,
    skip_gain,
    mamba_gain,
    keys_values,
    attn_gain,
    documents,
    placement_perm,
):
    devices = lax.axis_size("ctx")
    myself = lax.axis_index("ctx")
    tok_rows = mixer_input.shape[1]
    kv_cols = keys_values.shape[2]
    halves = KVHEADS
    half_heads = HEADS // halves
    half_groups = GROUPS // halves
    half_cols = half_heads * HEAD_DIM
    share = devices // half_heads
    slot_rows = HEAD_DIM // share
    kv_half = kv_cols // halves
    slice_cols = kv_half // devices
    kv_rows = tok_rows * slice_cols // LANES

    inverse = (
        jnp.zeros((devices,), jnp.int32)
        .at[placement_perm]
        .set(jnp.arange(devices, dtype=jnp.int32))
    )
    segment = documents[0]
    block_seg = segment.reshape(devices, tok_rows)
    seg_end = block_seg[:, -1]
    seg_prev = jnp.concatenate([jnp.full((1,), -1, jnp.int32), seg_end[:-1]])
    my_block = placement_perm[myself]
    my_seg = lax.dynamic_slice_in_dim(segment, my_block * tok_rows, tok_rows, 0)
    my_prev = seg_prev[my_block]
    positions = jnp.arange(devices)
    linked = (positions[None, :] < positions[:, None]) & (seg_end[None, :] == seg_prev[:, None])
    halo_blocks = placement_perm[:, None] - HALO + jnp.arange(HALO)[None, :]
    halo_src = inverse[jnp.clip(halo_blocks, 0, devices - 1)]

    query_pos = my_block * tok_rows + jnp.arange(tok_rows, dtype=jnp.int32)
    key_pos = (my_block - HALO) * tok_rows + jnp.arange((HALO + 1) * tok_rows, dtype=jnp.int32)
    key_seg = jnp.take(segment, jnp.maximum(key_pos, 0))
    allowed = (
        (my_seg[:, None] == key_seg[None, :])
        & (key_pos[None, :] <= query_pos[:, None])
        & (key_pos[None, :] >= 0)
    )
    score_scale = 1.0 / math.sqrt(QDIM)

    inputs = mixer_input[0]
    projections = state_proj[0]
    raw_all = dt_raw[0]
    kv = keys_values[0]
    my_head = myself // share
    my_part = myself % share

    hidden_parts = []
    attended_parts = []
    for half in range(halves):
        cols = slice(half * half_cols, (half + 1) * half_cols)
        heads = slice(half * half_heads, (half + 1) * half_heads)
        x_half = inputs[:, cols]
        values = x_half.astype(jnp.float32).reshape(tok_rows, half_heads, HEAD_DIM)
        paired = projections[:, half * half_groups * 2 * STATE : (half + 1) * half_groups * 2 * STATE]
        paired = paired.reshape(tok_rows, half_groups, 2, STATE)
        inject = paired[:, :, 0]
        readout = paired[:, :, 1]
        raw_half = raw_all[:, heads]
        step_sizes = jax.nn.softplus(raw_half.astype(jnp.float32) + dt_bias[0][heads])
        local_out, states, cum_log = block_terms(
            values, inject, readout, step_sizes, decay_rate[0][heads], my_seg
        )

        state_slots = states.astype(jnp.bfloat16).reshape(devices, slot_rows, STATE)
        kv_here = jnp.concatenate(
            [
                kv[:, half * QDIM : (half + 1) * QDIM],
                kv[:, kv_half + half * QDIM : kv_half + (half + 1) * QDIM],
            ],
            axis=1,
        )
        kv_slices = kv_here.reshape(tok_rows, devices, slice_cols).transpose(1, 0, 2)
        kv_slices = kv_slices.reshape(devices, kv_rows, LANES)
        raw_cols = jnp.repeat(raw_half.T, share, axis=0).reshape(devices, 1, tok_rows)
        used = slot_rows + kv_rows + 1
        padding = jnp.zeros((devices, -used % 8, LANES), jnp.bfloat16)
        first = jnp.concatenate([state_slots, kv_slices, raw_cols, padding], axis=1)
        got = lax.all_to_all(first, "ctx", split_axis=0, concat_axis=0, tiled=True)
        got_states = got[:, :slot_rows].astype(jnp.float32)
        got_kv = got[:, slot_rows : slot_rows + kv_rows]
        got_raw = got[:, slot_rows + kv_rows].astype(jnp.float32)

        head_id = half * half_heads + my_head
        my_rate = decay_rate[0][head_id]
        my_bias = dt_bias[0][head_id]
        my_steps = jax.nn.softplus(got_raw + my_bias)
        endings = jnp.cumsum(-my_rate * my_steps, axis=1)[:, -1]
        ending_pos = endings[inverse]
        running = jnp.cumsum(ending_pos)
        before = running - ending_pos
        factors = jnp.where(
            linked, jnp.exp(jnp.minimum(before[:, None] - running[None, :], 0.0)), 0.0
        )
        by_device = factors[placement_perm][:, placement_perm]
        entering = jnp.einsum("ds,spn->dpn", by_device, got_states, precision=precise)

        halo = got_kv[halo_src].reshape(devices, HALO * kv_rows, LANES)
        second = jnp.concatenate([entering.astype(jnp.bfloat16), halo], axis=1)
        back = lax.all_to_all(second, "ctx", split_axis=0, concat_axis=0, tiled=True)
        enter_here = back[:, :slot_rows].reshape(
            half_groups, half_heads // half_groups, HEAD_DIM, STATE
        )
        halo_here = back[:, slot_rows:].reshape(devices, HALO * tok_rows, slice_cols)
        halo_kv = halo_here.transpose(1, 0, 2).reshape(HALO * tok_rows, kv_half)

        reach = jnp.where((my_seg == my_prev)[:, None], jnp.exp(cum_log), 0.0)
        read_out = jnp.einsum(
            "tgs,gkps->tgkp", readout, enter_here, preferred_element_type=jnp.float32
        ).reshape(tok_rows, half_heads, HEAD_DIM)
        outputs = local_out + read_out * reach[..., None] + skip_gain[0][heads][:, None] * values
        mamba_out = outputs.astype(jnp.bfloat16).reshape(tok_rows, half_cols)
        residual = x_half.astype(jnp.float32) + group_norm(
            mamba_out.astype(jnp.float32), mamba_gain[0][cols]
        )
        hidden = residual.astype(jnp.bfloat16)
        hidden_parts.append(hidden)

        queries = hidden.reshape(tok_rows, half_cols // QDIM, QDIM)
        all_kv = jnp.concatenate([halo_kv, kv_here], axis=0)
        keys = all_kv[:, :QDIM]
        vals = all_kv[:, QDIM:]
        logits = (
            jnp.einsum("trd,kd->rtk", queries, keys, preferred_element_type=jnp.float32)
            * score_scale
        )
        logits = jnp.where(allowed, logits, -1e30)
        best = jnp.max(logits, axis=-1, keepdims=True)
        weights = jnp.where(allowed, jnp.exp(logits - best), 0.0)
        total_weight = jnp.sum(weights, axis=-1)
        blended = jnp.einsum(
            "rtk,kd->rtd", weights.astype(jnp.bfloat16), vals, preferred_element_type=jnp.float32
        )
        attended = (blended / total_weight[..., None]).transpose(1, 0, 2).reshape(tok_rows, half_cols)
        attended_parts.append(attended)

    hidden = jnp.concatenate(hidden_parts, axis=1)
    attended = jnp.concatenate(attended_parts, axis=1)
    normed = (
        attended
        * lax.rsqrt(jnp.mean(attended * attended, axis=-1, keepdims=True) + epsilon)
        * attn_gain[0]
    )
    result = (hidden.astype(jnp.float32) + normed).astype(jnp.bfloat16)
    return passed_along(result[None], "phase", 1)


def solution(mesh):
    in_specs = (
        P("phase", "ctx", None),
        P("phase", "ctx", None),
        P("phase", "ctx", None),
        P("phase", None),
        P("phase", None),
        P("phase", None),
        P("phase", None),
        P("phase", "ctx", None),
        P("phase", None),
        P("phase", None),
        P(),
    )
    out_specs = P("phase", "ctx", None)
    return jax.shard_map(
        on_device, mesh=mesh, in_specs=in_specs, out_specs=out_specs, check_vma=False
    )
```

```python
import math

import jax
import jax.numpy as jnp
from jax import lax
from jax.sharding import PartitionSpec as P

HEADS = 64
HEAD_DIM = 64
GROUPS = 8
STATE = 128
QHEADS = 32
KVHEADS = 2
QDIM = 128
HALO = 4


precise = lax.Precision.HIGHEST
epsilon = 1e-05


def passed_along(value, axis, steps):
    count = lax.axis_size(axis)
    pairs = [(source, (source + steps) % count) for source in range(count)]
    return lax.ppermute(value, axis, pairs)


def group_norm(values, gain):
    grouped = values.reshape(values.shape[0], GROUPS, -1)
    normed = grouped * lax.rsqrt(jnp.mean(grouped * grouped, axis=-1, keepdims=True) + epsilon)
    return normed.reshape(values.shape) * gain


def block_terms(values, inject, readout, step_sizes, rates, seg):
    length = values.shape[0]
    within = HEADS // GROUPS
    cum_log = jnp.cumsum(-rates * step_sizes, axis=0)
    positions = jnp.arange(length)
    allowed = (positions[:, None] >= positions[None, :]) & (seg[:, None] == seg[None, :])
    spread = cum_log.T[:, :, None] - cum_log.T[:, None, :]
    decays = jnp.where(allowed[None], jnp.exp(jnp.minimum(spread, 0.0)), 0.0)
    scores = jnp.einsum("tgs,ugs->gtu", readout, inject, preferred_element_type=jnp.float32)
    weights = decays.reshape(GROUPS, within, length, length) * scores[:, None]
    scaled = values * step_sizes[..., None]
    local_out = jnp.einsum(
        "gktu,ugkp->tgkp",
        weights,
        scaled.reshape(length, GROUPS, within, HEAD_DIM),
        precision=precise,
    ).reshape(values.shape)
    ending = cum_log[-1]
    to_end = jnp.where((seg == seg[-1])[:, None], jnp.exp(ending[None, :] - cum_log), 0.0)
    weighted = (scaled * to_end[..., None]).reshape(length, GROUPS, within, HEAD_DIM)
    states = jnp.einsum(
        "tgkp,tgs->gkps", weighted, inject.astype(jnp.float32), precision=precise
    ).reshape(HEADS, HEAD_DIM, STATE)
    return local_out, states, cum_log, ending


def on_device(
    mixer_input,
    state_proj,
    dt_raw,
    decay_rate,
    dt_bias,
    skip_gain,
    mamba_gain,
    keys_values,
    attn_gain,
    documents,
    placement_perm,
):
    devices = lax.axis_size("ctx")
    myself = lax.axis_index("ctx")
    tok_rows = mixer_input.shape[1]
    kv_cols = keys_values.shape[2]
    slice_cols = kv_cols // devices
    inverse = (
        jnp.zeros((devices,), jnp.int32)
        .at[placement_perm]
        .set(jnp.arange(devices, dtype=jnp.int32))
    )
    segment = documents[0]
    block_seg = segment.reshape(devices, tok_rows)
    seg_end = block_seg[:, -1]
    seg_prev = jnp.concatenate([jnp.full((1,), -1, jnp.int32), seg_end[:-1]])
    my_block = placement_perm[myself]
    my_seg = lax.dynamic_slice_in_dim(segment, my_block * tok_rows, tok_rows, 0)
    my_prev = seg_prev[my_block]

    inputs = mixer_input[0]
    values = inputs.astype(jnp.float32).reshape(tok_rows, HEADS, HEAD_DIM)
    paired = state_proj[0].reshape(tok_rows, GROUPS, 2, STATE)
    inject = paired[:, :, 0]
    readout = paired[:, :, 1]
    step_sizes = jax.nn.softplus(dt_raw[0].astype(jnp.float32) + dt_bias[0])
    local_out, states, cum_log, ending = block_terms(
        values, inject, readout, step_sizes, decay_rate[0], my_seg
    )

    kv = keys_values[0]
    lanes = 128
    share = tok_rows // devices
    kv_rows = share * kv_cols // lanes
    kv_slices = kv.reshape(devices, kv_rows, lanes)
    raw_cols = dt_raw[0].T.reshape(HEADS, 1, tok_rows)
    state_slots = states.astype(jnp.bfloat16)
    used = HEAD_DIM + kv_rows + 1
    padding = jnp.zeros((devices, -used % 8, lanes), jnp.bfloat16)
    first = jnp.concatenate([state_slots, kv_slices, raw_cols, padding], axis=1)
    got = lax.all_to_all(first, "ctx", split_axis=0, concat_axis=0, tiled=True)
    got_states = got[:, :HEAD_DIM].astype(jnp.float32)
    got_kv = got[:, HEAD_DIM : HEAD_DIM + kv_rows]
    got_raw = got[:, HEAD_DIM + kv_rows].astype(jnp.float32)

    my_rate = decay_rate[0][myself]
    my_bias = dt_bias[0][myself]
    my_steps = jax.nn.softplus(got_raw + my_bias)
    endings = jnp.cumsum(-my_rate * my_steps, axis=1)[:, -1]
    ending_pos = endings[inverse]
    running = jnp.cumsum(ending_pos)
    before = running - ending_pos
    positions = jnp.arange(devices)
    linked = (positions[None, :] < positions[:, None]) & (seg_end[None, :] == seg_prev[:, None])
    factors = jnp.where(
        linked, jnp.exp(jnp.minimum(before[:, None] - running[None, :], 0.0)), 0.0
    )
    by_device = factors[placement_perm][:, placement_perm]
    entering = jnp.einsum("ds,spn->dpn", by_device, got_states, precision=precise)

    halo_blocks = placement_perm[:, None] - HALO + jnp.arange(HALO)[None, :]
    halo_src = inverse[jnp.clip(halo_blocks, 0, devices - 1)]
    halo = got_kv[halo_src].reshape(devices, HALO * kv_rows, lanes)
    second = jnp.concatenate([entering.astype(jnp.bfloat16), halo], axis=1)
    back = lax.all_to_all(second, "ctx", split_axis=0, concat_axis=0, tiled=True)
    enter_here = back[:, :HEAD_DIM].reshape(GROUPS, HEADS // GROUPS, HEAD_DIM, STATE)
    halo_kv = back[:, HEAD_DIM:].reshape(devices * HALO * share, kv_cols)
    halo_pos = (
        (my_block - HALO + jnp.arange(HALO))[None, :, None] * tok_rows
        + share * jnp.arange(devices)[:, None, None]
        + jnp.arange(share)[None, None, :]
    ).reshape(-1)

    reach = jnp.where((my_seg == my_prev)[:, None], jnp.exp(cum_log), 0.0)
    read_out = jnp.einsum(
        "tgs,gkps->tgkp", readout, enter_here, preferred_element_type=jnp.float32
    ).reshape(tok_rows, HEADS, HEAD_DIM)
    outputs = local_out + read_out * reach[..., None] + skip_gain[0][:, None] * values
    mamba_out = outputs.astype(jnp.bfloat16).reshape(tok_rows, HEADS * HEAD_DIM)
    residual = inputs.astype(jnp.float32) + group_norm(mamba_out.astype(jnp.float32), mamba_gain[0])
    hidden = residual.astype(jnp.bfloat16)

    repeat = QHEADS // KVHEADS
    all_kv = jnp.concatenate([halo_kv, kv], axis=0).reshape(-1, 2, KVHEADS, QDIM)
    keys = all_kv[:, 0]
    vals = all_kv[:, 1]
    key_pos = jnp.concatenate(
        [halo_pos, my_block * tok_rows + jnp.arange(tok_rows, dtype=jnp.int32)]
    )
    key_seg = jnp.take(segment, jnp.maximum(key_pos, 0))
    score_scale = 1.0 / math.sqrt(QDIM)
    pieces = 2
    rows = tok_rows // pieces
    handed = []
    for piece in range(pieces):
        part = slice(piece * rows, (piece + 1) * rows)
        hidden_part = hidden[part]
        if handed:
            hidden_part, _ = lax.optimization_barrier((hidden_part, result))
        queries = hidden_part.reshape(rows, KVHEADS, repeat, QDIM)
        query_pos = my_block * tok_rows + piece * rows + jnp.arange(rows, dtype=jnp.int32)
        allowed = (
            (my_seg[part][:, None] == key_seg[None, :])
            & (key_pos[None, :] <= query_pos[:, None])
            & (key_pos[None, :] >= 0)
        )
        logits = (
            jnp.einsum("tgrd,kgd->grtk", queries, keys, preferred_element_type=jnp.float32)
            * score_scale
        )
        logits = jnp.where(allowed, logits, -1e30)
        best = jnp.max(logits, axis=-1, keepdims=True)
        weights = jnp.where(allowed, jnp.exp(logits - best), 0.0)
        total_weight = jnp.sum(weights, axis=-1)
        blended = jnp.einsum(
            "grtk,kgd->grtd", weights.astype(jnp.bfloat16), vals, preferred_element_type=jnp.float32
        )
        attended = (
            (blended / total_weight[..., None]).transpose(2, 0, 1, 3).reshape(rows, QHEADS * QDIM)
        )
        normed = (
            attended
            * lax.rsqrt(jnp.mean(attended * attended, axis=-1, keepdims=True) + epsilon)
            * attn_gain[0]
        )
        result = (hidden_part.astype(jnp.float32) + normed).astype(jnp.bfloat16)
        handed.append(passed_along(result[None], "phase", 1))
    return jnp.concatenate(handed, axis=1)


def solution(mesh):
    in_specs = (
        P("phase", "ctx", None),
        P("phase", "ctx", None),
        P("phase", "ctx", None),
        P("phase", None),
        P("phase", None),
        P("phase", None),
        P("phase", None),
        P("phase", "ctx", None),
        P("phase", None),
        P("phase", None),
        P(),
    )
    out_specs = P("phase", "ctx", None)
    return jax.shard_map(
        on_device, mesh=mesh, in_specs=in_specs, out_specs=out_specs, check_vma=False
    )
```

```python
import math

import jax
import jax.numpy as jnp
from jax import lax
from jax.sharding import PartitionSpec as P

HEADS = 64
HEAD_DIM = 64
GROUPS = 8
STATE = 128
QHEADS = 32
KVHEADS = 2
QDIM = 128
HALO = 4


precise = lax.Precision.HIGHEST
epsilon = 1e-05


def passed_along(value, axis, steps):
    count = lax.axis_size(axis)
    pairs = [(source, (source + steps) % count) for source in range(count)]
    return lax.ppermute(value, axis, pairs)


def group_norm(values, gain):
    grouped = values.reshape(values.shape[0], GROUPS, -1)
    normed = grouped * lax.rsqrt(jnp.mean(grouped * grouped, axis=-1, keepdims=True) + epsilon)
    return normed.reshape(values.shape) * gain


def block_terms(values, inject, readout, step_sizes, rates, seg):
    length = values.shape[0]
    within = HEADS // GROUPS
    cum_log = jnp.cumsum(-rates * step_sizes, axis=0)
    positions = jnp.arange(length)
    allowed = (positions[:, None] >= positions[None, :]) & (seg[:, None] == seg[None, :])
    spread = cum_log.T[:, :, None] - cum_log.T[:, None, :]
    decays = jnp.where(allowed[None], jnp.exp(jnp.minimum(spread, 0.0)), 0.0)
    scores = jnp.einsum("tgs,ugs->gtu", readout, inject, preferred_element_type=jnp.float32)
    weights = decays.reshape(GROUPS, within, length, length) * scores[:, None]
    scaled = values * step_sizes[..., None]
    local_out = jnp.einsum(
        "gktu,ugkp->tgkp",
        weights,
        scaled.reshape(length, GROUPS, within, HEAD_DIM),
        precision=precise,
    ).reshape(values.shape)
    ending = cum_log[-1]
    to_end = jnp.where((seg == seg[-1])[:, None], jnp.exp(ending[None, :] - cum_log), 0.0)
    weighted = (scaled * to_end[..., None]).reshape(length, GROUPS, within, HEAD_DIM)
    states = jnp.einsum(
        "tgkp,tgs->gkps", weighted, inject.astype(jnp.float32), precision=precise
    ).reshape(HEADS, HEAD_DIM, STATE)
    return local_out, states, cum_log, ending


def on_device(
    mixer_input,
    state_proj,
    dt_raw,
    decay_rate,
    dt_bias,
    skip_gain,
    mamba_gain,
    keys_values,
    attn_gain,
    documents,
    placement_perm,
):
    devices = lax.axis_size("ctx")
    myself = lax.axis_index("ctx")
    tok_rows = mixer_input.shape[1]
    kv_cols = keys_values.shape[2]
    slice_cols = kv_cols // devices
    inverse = (
        jnp.zeros((devices,), jnp.int32)
        .at[placement_perm]
        .set(jnp.arange(devices, dtype=jnp.int32))
    )
    segment = documents[0]
    block_seg = segment.reshape(devices, tok_rows)
    seg_end = block_seg[:, -1]
    seg_prev = jnp.concatenate([jnp.full((1,), -1, jnp.int32), seg_end[:-1]])
    my_block = placement_perm[myself]
    my_seg = lax.dynamic_slice_in_dim(segment, my_block * tok_rows, tok_rows, 0)
    my_prev = seg_prev[my_block]

    inputs = mixer_input[0]
    values = inputs.astype(jnp.float32).reshape(tok_rows, HEADS, HEAD_DIM)
    paired = state_proj[0].reshape(tok_rows, GROUPS, 2, STATE)
    inject = paired[:, :, 0]
    readout = paired[:, :, 1]
    step_sizes = jax.nn.softplus(dt_raw[0].astype(jnp.float32) + dt_bias[0])
    local_out, states, cum_log, ending = block_terms(
        values, inject, readout, step_sizes, decay_rate[0], my_seg
    )

    kv = keys_values[0]
    lanes = 128
    share = tok_rows // devices
    kv_rows = share * kv_cols // lanes
    kv_slices = kv.reshape(devices, kv_rows, lanes)
    raw_cols = dt_raw[0].T.reshape(HEADS, 1, tok_rows)
    state_slots = states.astype(jnp.bfloat16)
    used = HEAD_DIM + kv_rows + 1
    padding = jnp.zeros((devices, -used % 8, lanes), jnp.bfloat16)
    first = jnp.concatenate([state_slots, kv_slices, raw_cols, padding], axis=1)
    got = lax.all_to_all(first, "ctx", split_axis=0, concat_axis=0, tiled=True)
    got_states = got[:, :HEAD_DIM].astype(jnp.float32)
    got_kv = got[:, HEAD_DIM : HEAD_DIM + kv_rows]
    got_raw = got[:, HEAD_DIM + kv_rows].astype(jnp.float32)

    my_rate = decay_rate[0][myself]
    my_bias = dt_bias[0][myself]
    my_steps = jax.nn.softplus(got_raw + my_bias)
    endings = jnp.cumsum(-my_rate * my_steps, axis=1)[:, -1]
    ending_pos = endings[inverse]
    running = jnp.cumsum(ending_pos)
    before = running - ending_pos
    positions = jnp.arange(devices)
    linked = (positions[None, :] < positions[:, None]) & (seg_end[None, :] == seg_prev[:, None])
    factors = jnp.where(
        linked, jnp.exp(jnp.minimum(before[:, None] - running[None, :], 0.0)), 0.0
    )
    by_device = factors[placement_perm][:, placement_perm]
    entering = jnp.einsum("ds,spn->dpn", by_device, got_states, precision=precise)

    halo_blocks = placement_perm[:, None] - HALO + jnp.arange(HALO)[None, :]
    halo_src = inverse[jnp.clip(halo_blocks, 0, devices - 1)]
    halo = got_kv[halo_src].reshape(devices, HALO * kv_rows, lanes)
    second = jnp.concatenate([entering.astype(jnp.bfloat16), halo], axis=1)
    back = lax.all_to_all(second, "ctx", split_axis=0, concat_axis=0, tiled=True)
    enter_here = back[:, :HEAD_DIM].reshape(GROUPS, HEADS // GROUPS, HEAD_DIM, STATE)
    halo_kv = back[:, HEAD_DIM:].reshape(devices * HALO * share, kv_cols)
    halo_pos = (
        (my_block - HALO + jnp.arange(HALO))[None, :, None] * tok_rows
        + share * jnp.arange(devices)[:, None, None]
        + jnp.arange(share)[None, None, :]
    ).reshape(-1)

    reach = jnp.where((my_seg == my_prev)[:, None], jnp.exp(cum_log), 0.0)
    read_out = jnp.einsum(
        "tgs,gkps->tgkp", readout, enter_here, preferred_element_type=jnp.float32
    ).reshape(tok_rows, HEADS, HEAD_DIM)
    outputs = local_out + read_out * reach[..., None] + skip_gain[0][:, None] * values
    mamba_out = outputs.astype(jnp.bfloat16).reshape(tok_rows, HEADS * HEAD_DIM)
    residual = inputs.astype(jnp.float32) + group_norm(mamba_out.astype(jnp.float32), mamba_gain[0])
    hidden = residual.astype(jnp.bfloat16)

    repeat = QHEADS // KVHEADS
    all_kv = jnp.concatenate([halo_kv, kv], axis=0)
    key_pos = jnp.concatenate(
        [halo_pos, my_block * tok_rows + jnp.arange(tok_rows, dtype=jnp.int32)]
    )
    key_seg = jnp.take(segment, jnp.maximum(key_pos, 0))
    score_scale = 1.0 / math.sqrt(QDIM)
    kv_width = KVHEADS * QDIM
    pieces = 2
    rows = tok_rows // pieces
    handed = []
    for piece in range(pieces):
        part = slice(piece * rows, (piece + 1) * rows)
        hidden_part = hidden[part]
        if handed:
            hidden_part, _ = lax.optimization_barrier((hidden_part, result))
        query_pos = my_block * tok_rows + piece * rows + jnp.arange(rows, dtype=jnp.int32)
        allowed = (
            (my_seg[part][:, None] == key_seg[None, :])
            & (key_pos[None, :] <= query_pos[:, None])
            & (key_pos[None, :] >= 0)
        )
        heads_out = []
        for kv_head in range(KVHEADS):
            queries = hidden_part[:, kv_head * repeat * QDIM : (kv_head + 1) * repeat * QDIM]
            queries = queries.reshape(rows, repeat, QDIM)
            keys = all_kv[:, kv_head * QDIM : (kv_head + 1) * QDIM]
            vals = all_kv[:, kv_width + kv_head * QDIM : kv_width + (kv_head + 1) * QDIM]
            logits = (
                jnp.einsum("trd,kd->trk", queries, keys, preferred_element_type=jnp.float32)
                * score_scale
            )
            logits = jnp.where(allowed[:, None, :], logits, -1e30)
            best = jnp.max(logits, axis=-1, keepdims=True)
            weights = jnp.where(allowed[:, None, :], jnp.exp(logits - best), 0.0)
            total_weight = jnp.sum(weights, axis=-1)
            blended = jnp.einsum(
                "trk,kd->trd", weights.astype(jnp.bfloat16), vals, preferred_element_type=jnp.float32
            )
            heads_out.append((blended / total_weight[..., None]).reshape(rows, repeat * QDIM))
        attended = jnp.concatenate(heads_out, axis=1)
        normed = (
            attended
            * lax.rsqrt(jnp.mean(attended * attended, axis=-1, keepdims=True) + epsilon)
            * attn_gain[0]
        )
        result = (hidden_part.astype(jnp.float32) + normed).astype(jnp.bfloat16)
        handed.append(passed_along(result[None], "phase", 1))
    return jnp.concatenate(handed, axis=1)


def solution(mesh):
    in_specs = (
        P("phase", "ctx", None),
        P("phase", "ctx", None),
        P("phase", "ctx", None),
        P("phase", None),
        P("phase", None),
        P("phase", None),
        P("phase", None),
        P("phase", "ctx", None),
        P("phase", None),
        P("phase", None),
        P(),
    )
    out_specs = P("phase", "ctx", None)
    return jax.shard_map(
        on_device, mesh=mesh, in_specs=in_specs, out_specs=out_specs, check_vma=False
    )
```

```python
import math

import jax
import jax.numpy as jnp
from jax import lax
from jax.experimental import pallas as pl
from jax.experimental.pallas import tpu as pltpu
from jax.sharding import PartitionSpec as P

HEADS = 64
HEAD_DIM = 64
GROUPS = 8
STATE = 128
QHEADS = 32
KVHEADS = 2
QDIM = 128
HALO = 4


precise = lax.Precision.HIGHEST
epsilon = 1e-05


def passed_along(value, axis, steps):
    count = lax.axis_size(axis)
    pairs = [(source, (source + steps) % count) for source in range(count)]
    return lax.ppermute(value, axis, pairs)


def group_norm(values, gain):
    grouped = values.reshape(values.shape[0], GROUPS, -1)
    normed = grouped * lax.rsqrt(jnp.mean(grouped * grouped, axis=-1, keepdims=True) + epsilon)
    return normed.reshape(values.shape) * gain


def block_terms(values, inject, readout, step_sizes, rates, seg):
    length = values.shape[0]
    within = HEADS // GROUPS
    cum_log = jnp.cumsum(-rates * step_sizes, axis=0)
    positions = jnp.arange(length)
    allowed = (positions[:, None] >= positions[None, :]) & (seg[:, None] == seg[None, :])
    spread = cum_log.T[:, :, None] - cum_log.T[:, None, :]
    decays = jnp.where(allowed[None], jnp.exp(jnp.minimum(spread, 0.0)), 0.0)
    scores = jnp.einsum("tgs,ugs->gtu", readout, inject, preferred_element_type=jnp.float32)
    weights = decays.reshape(GROUPS, within, length, length) * scores[:, None]
    scaled = values * step_sizes[..., None]
    local_out = jnp.einsum(
        "gktu,ugkp->tgkp",
        weights,
        scaled.reshape(length, GROUPS, within, HEAD_DIM),
        precision=precise,
    ).reshape(values.shape)
    ending = cum_log[-1]
    to_end = jnp.where((seg == seg[-1])[:, None], jnp.exp(ending[None, :] - cum_log), 0.0)
    weighted = (scaled * to_end[..., None]).reshape(length, GROUPS, within, HEAD_DIM)
    states = jnp.einsum(
        "tgkp,tgs->gkps", weighted, inject.astype(jnp.float32), precision=precise
    ).reshape(HEADS, HEAD_DIM, STATE)
    return local_out, states, cum_log, ending


def attention_kernel(q_ref, kv_ref, qpos_ref, qseg_ref, kpos_ref, kseg_ref, gain_ref, out_ref, acc_ref):
    repeat = QHEADS // KVHEADS
    kv_width = KVHEADS * QDIM
    score_scale = 1.0 / math.sqrt(QDIM)
    allowed = (
        (qseg_ref[...] == kseg_ref[...])
        & (kpos_ref[...] <= qpos_ref[...])
        & (kpos_ref[...] >= 0)
    )

    def one_head(head, squares):
        group = head // repeat
        q = q_ref[:, pl.ds(pl.multiple_of(head * QDIM, QDIM), QDIM)]
        k = kv_ref[:, pl.ds(pl.multiple_of(group * QDIM, QDIM), QDIM)]
        v = kv_ref[:, pl.ds(pl.multiple_of(kv_width + group * QDIM, QDIM), QDIM)]
        logits = (
            lax.dot_general(q, k, (((1,), (1,)), ((), ())), preferred_element_type=jnp.float32)
            * score_scale
        )
        logits = jnp.where(allowed, logits, -1e30)
        best = jnp.max(logits, axis=-1, keepdims=True)
        weights = jnp.where(allowed, jnp.exp(logits - best), 0.0)
        total = jnp.sum(weights, axis=-1, keepdims=True)
        blended = jnp.dot(weights.astype(jnp.bfloat16), v, preferred_element_type=jnp.float32)
        attended = blended / total
        acc_ref[:, pl.ds(pl.multiple_of(head * QDIM, QDIM), QDIM)] = attended
        return squares + jnp.sum(attended * attended, axis=-1, keepdims=True)

    squares = lax.fori_loop(0, QHEADS, one_head, jnp.zeros((q_ref.shape[0], 1), jnp.float32))
    scale = lax.rsqrt(squares / (QHEADS * QDIM) + epsilon)
    out_ref[...] = (
        q_ref[...].astype(jnp.float32) + acc_ref[...] * scale * gain_ref[...]
    ).astype(out_ref.dtype)


def attention_block(hidden_part, all_kv, query_pos, query_seg, key_pos, key_seg, gain):
    rows = hidden_part.shape[0]
    keys = all_kv.shape[0]
    flops = 4 * rows * keys * QDIM * QHEADS
    return pl.pallas_call(
        attention_kernel,
        out_shape=jax.ShapeDtypeStruct(hidden_part.shape, jnp.bfloat16),
        scratch_shapes=[pltpu.VMEM(hidden_part.shape, jnp.float32)],
        cost_estimate=pl.CostEstimate(
            flops=flops,
            transcendentals=rows * keys * QHEADS,
            bytes_accessed=2 * hidden_part.size * 2 + all_kv.size * 2,
        ),
    )(
        hidden_part,
        all_kv,
        query_pos.reshape(rows, 1),
        query_seg.reshape(rows, 1),
        key_pos.reshape(1, keys),
        key_seg.reshape(1, keys),
        gain.reshape(1, -1),
    )


def on_device(
    mixer_input,
    state_proj,
    dt_raw,
    decay_rate,
    dt_bias,
    skip_gain,
    mamba_gain,
    keys_values,
    attn_gain,
    documents,
    placement_perm,
):
    devices = lax.axis_size("ctx")
    myself = lax.axis_index("ctx")
    tok_rows = mixer_input.shape[1]
    kv_cols = keys_values.shape[2]
    slice_cols = kv_cols // devices
    inverse = (
        jnp.zeros((devices,), jnp.int32)
        .at[placement_perm]
        .set(jnp.arange(devices, dtype=jnp.int32))
    )
    segment = documents[0]
    block_seg = segment.reshape(devices, tok_rows)
    seg_end = block_seg[:, -1]
    seg_prev = jnp.concatenate([jnp.full((1,), -1, jnp.int32), seg_end[:-1]])
    my_block = placement_perm[myself]
    my_seg = lax.dynamic_slice_in_dim(segment, my_block * tok_rows, tok_rows, 0)
    my_prev = seg_prev[my_block]

    inputs = mixer_input[0]
    values = inputs.astype(jnp.float32).reshape(tok_rows, HEADS, HEAD_DIM)
    paired = state_proj[0].reshape(tok_rows, GROUPS, 2, STATE)
    inject = paired[:, :, 0]
    readout = paired[:, :, 1]
    step_sizes = jax.nn.softplus(dt_raw[0].astype(jnp.float32) + dt_bias[0])
    local_out, states, cum_log, ending = block_terms(
        values, inject, readout, step_sizes, decay_rate[0], my_seg
    )

    kv = keys_values[0]
    lanes = 128
    share = tok_rows // devices
    kv_rows = share * kv_cols // lanes
    kv_slices = kv.reshape(devices, kv_rows, lanes)
    raw_cols = dt_raw[0].T.reshape(HEADS, 1, tok_rows)
    state_slots = states.astype(jnp.bfloat16)
    used = HEAD_DIM + kv_rows + 1
    padding = jnp.zeros((devices, -used % 8, lanes), jnp.bfloat16)
    first = jnp.concatenate([state_slots, kv_slices, raw_cols, padding], axis=1)
    got = lax.all_to_all(first, "ctx", split_axis=0, concat_axis=0, tiled=True)
    got_states = got[:, :HEAD_DIM].astype(jnp.float32)
    got_kv = got[:, HEAD_DIM : HEAD_DIM + kv_rows]
    got_raw = got[:, HEAD_DIM + kv_rows].astype(jnp.float32)

    my_rate = decay_rate[0][myself]
    my_bias = dt_bias[0][myself]
    my_steps = jax.nn.softplus(got_raw + my_bias)
    endings = jnp.cumsum(-my_rate * my_steps, axis=1)[:, -1]
    ending_pos = endings[inverse]
    running = jnp.cumsum(ending_pos)
    before = running - ending_pos
    positions = jnp.arange(devices)
    linked = (positions[None, :] < positions[:, None]) & (seg_end[None, :] == seg_prev[:, None])
    factors = jnp.where(
        linked, jnp.exp(jnp.minimum(before[:, None] - running[None, :], 0.0)), 0.0
    )
    by_device = factors[placement_perm][:, placement_perm]
    entering = jnp.einsum("ds,spn->dpn", by_device, got_states, precision=precise)

    halo_blocks = placement_perm[:, None] - HALO + jnp.arange(HALO)[None, :]
    halo_src = inverse[jnp.clip(halo_blocks, 0, devices - 1)]
    halo = got_kv[halo_src].reshape(devices, HALO * kv_rows, lanes)
    second = jnp.concatenate([entering.astype(jnp.bfloat16), halo], axis=1)
    back = lax.all_to_all(second, "ctx", split_axis=0, concat_axis=0, tiled=True)
    enter_here = back[:, :HEAD_DIM].reshape(GROUPS, HEADS // GROUPS, HEAD_DIM, STATE)
    halo_kv = back[:, HEAD_DIM:].reshape(devices * HALO * share, kv_cols)
    halo_pos = (
        (my_block - HALO + jnp.arange(HALO))[None, :, None] * tok_rows
        + share * jnp.arange(devices)[:, None, None]
        + jnp.arange(share)[None, None, :]
    ).reshape(-1)

    reach = jnp.where((my_seg == my_prev)[:, None], jnp.exp(cum_log), 0.0)
    read_out = jnp.einsum(
        "tgs,gkps->tgkp", readout, enter_here, preferred_element_type=jnp.float32
    ).reshape(tok_rows, HEADS, HEAD_DIM)
    outputs = local_out + read_out * reach[..., None] + skip_gain[0][:, None] * values
    mamba_out = outputs.astype(jnp.bfloat16).reshape(tok_rows, HEADS * HEAD_DIM)
    residual = inputs.astype(jnp.float32) + group_norm(mamba_out.astype(jnp.float32), mamba_gain[0])
    hidden = residual.astype(jnp.bfloat16)

    all_kv_flat = jnp.concatenate([halo_kv, kv], axis=0)
    key_pos = jnp.concatenate(
        [halo_pos, my_block * tok_rows + jnp.arange(tok_rows, dtype=jnp.int32)]
    )
    key_seg = jnp.take(segment, jnp.maximum(key_pos, 0))
    pieces = 2
    rows = tok_rows // pieces
    handed = []
    for piece in range(pieces):
        part = slice(piece * rows, (piece + 1) * rows)
        hidden_part = hidden[part]
        if handed:
            hidden_part, _ = lax.optimization_barrier((hidden_part, result))
        query_pos = my_block * tok_rows + piece * rows + jnp.arange(rows, dtype=jnp.int32)
        result = attention_block(
            hidden_part, all_kv_flat, query_pos, my_seg[part], key_pos, key_seg, attn_gain[0]
        )
        handed.append(passed_along(result[None], "phase", 1))
    return jnp.concatenate(handed, axis=1)


def solution(mesh):
    in_specs = (
        P("phase", "ctx", None),
        P("phase", "ctx", None),
        P("phase", "ctx", None),
        P("phase", None),
        P("phase", None),
        P("phase", None),
        P("phase", None),
        P("phase", "ctx", None),
        P("phase", None),
        P("phase", None),
        P(),
    )
    out_specs = P("phase", "ctx", None)
    return jax.shard_map(
        on_device, mesh=mesh, in_specs=in_specs, out_specs=out_specs, check_vma=False
    )
```

```python
import math

import jax
import jax.numpy as jnp
from jax import lax
from jax.sharding import PartitionSpec as P

HEADS = 64
HEAD_DIM = 64
GROUPS = 8
STATE = 128
QHEADS = 32
KVHEADS = 2
QDIM = 128
HALO = 4


precise = lax.Precision.HIGHEST
epsilon = 1e-05


def passed_along(value, axis, steps):
    count = lax.axis_size(axis)
    pairs = [(source, (source + steps) % count) for source in range(count)]
    return lax.ppermute(value, axis, pairs)


def group_norm(values, gain):
    grouped = values.reshape(values.shape[0], GROUPS, -1)
    normed = grouped * lax.rsqrt(jnp.mean(grouped * grouped, axis=-1, keepdims=True) + epsilon)
    return normed.reshape(values.shape) * gain


def block_terms(values, inject, readout, step_sizes, rates, seg):
    length = values.shape[0]
    within = HEADS // GROUPS
    cum_log = jnp.cumsum(-rates * step_sizes, axis=0)
    positions = jnp.arange(length)
    allowed = (positions[:, None] >= positions[None, :]) & (seg[:, None] == seg[None, :])
    spread = cum_log.T[:, :, None] - cum_log.T[:, None, :]
    decays = jnp.where(allowed[None], jnp.exp(jnp.minimum(spread, 0.0)), 0.0)
    scores = jnp.einsum("tgs,ugs->gtu", readout, inject, preferred_element_type=jnp.float32)
    weights = decays.reshape(GROUPS, within, length, length) * scores[:, None]
    scaled = values * step_sizes[..., None]
    local_out = jnp.einsum(
        "gktu,ugkp->tgkp",
        weights,
        scaled.reshape(length, GROUPS, within, HEAD_DIM),
        precision=precise,
    ).reshape(values.shape)
    ending = cum_log[-1]
    to_end = jnp.where((seg == seg[-1])[:, None], jnp.exp(ending[None, :] - cum_log), 0.0)
    weighted = (scaled * to_end[..., None]).reshape(length, GROUPS, within, HEAD_DIM)
    states = jnp.einsum(
        "tgkp,tgs->gkps", weighted, inject.astype(jnp.float32), precision=precise
    ).reshape(HEADS, HEAD_DIM, STATE)
    return local_out, states, cum_log, ending


def on_device(
    mixer_input,
    state_proj,
    dt_raw,
    decay_rate,
    dt_bias,
    skip_gain,
    mamba_gain,
    keys_values,
    attn_gain,
    documents,
    placement_perm,
):
    devices = lax.axis_size("ctx")
    myself = lax.axis_index("ctx")
    tok_rows = mixer_input.shape[1]
    kv_cols = keys_values.shape[2]
    slice_cols = kv_cols // devices
    inverse = (
        jnp.zeros((devices,), jnp.int32)
        .at[placement_perm]
        .set(jnp.arange(devices, dtype=jnp.int32))
    )
    segment = documents[0]
    block_seg = segment.reshape(devices, tok_rows)
    seg_end = block_seg[:, -1]
    seg_prev = jnp.concatenate([jnp.full((1,), -1, jnp.int32), seg_end[:-1]])
    my_block = placement_perm[myself]
    my_seg = lax.dynamic_slice_in_dim(segment, my_block * tok_rows, tok_rows, 0)
    my_prev = seg_prev[my_block]

    inputs = mixer_input[0]
    values = inputs.astype(jnp.float32).reshape(tok_rows, HEADS, HEAD_DIM)
    paired = state_proj[0].reshape(tok_rows, GROUPS, 2, STATE)
    inject = paired[:, :, 0]
    readout = paired[:, :, 1]
    step_sizes = jax.nn.softplus(dt_raw[0].astype(jnp.float32) + dt_bias[0])
    local_out, states, cum_log, ending = block_terms(
        values, inject, readout, step_sizes, decay_rate[0], my_seg
    )

    kv = keys_values[0]
    lanes = 128
    share = tok_rows // devices
    kv_rows = share * kv_cols // lanes
    kv_slices = kv.reshape(devices, kv_rows, lanes)
    raw_cols = dt_raw[0].T.reshape(HEADS, 1, tok_rows)
    state_slots = states.astype(jnp.bfloat16)
    used = HEAD_DIM + kv_rows + 1
    padding = jnp.zeros((devices, -used % 8, lanes), jnp.bfloat16)
    first = jnp.concatenate([state_slots, kv_slices, raw_cols, padding], axis=1)
    got = lax.all_to_all(first, "ctx", split_axis=0, concat_axis=0, tiled=True)
    got_states = got[:, :HEAD_DIM].astype(jnp.float32)
    got_kv = got[:, HEAD_DIM : HEAD_DIM + kv_rows]
    got_raw = got[:, HEAD_DIM + kv_rows].astype(jnp.float32)

    my_rate = decay_rate[0][myself]
    my_bias = dt_bias[0][myself]
    my_steps = jax.nn.softplus(got_raw + my_bias)
    endings = jnp.cumsum(-my_rate * my_steps, axis=1)[:, -1]
    ending_pos = endings[inverse]
    running = jnp.cumsum(ending_pos)
    before = running - ending_pos
    positions = jnp.arange(devices)
    linked = (positions[None, :] < positions[:, None]) & (seg_end[None, :] == seg_prev[:, None])
    factors = jnp.where(
        linked, jnp.exp(jnp.minimum(before[:, None] - running[None, :], 0.0)), 0.0
    )
    by_device = factors[placement_perm][:, placement_perm]
    entering = jnp.einsum("ds,spn->dpn", by_device, got_states, precision=precise)

    halo_blocks = placement_perm[:, None] - HALO + jnp.arange(HALO)[None, :]
    halo_src = inverse[jnp.clip(halo_blocks, 0, devices - 1)]
    halo = got_kv[halo_src].reshape(devices, HALO * kv_rows, lanes)
    second = jnp.concatenate([entering.astype(jnp.bfloat16), halo], axis=1)
    back = lax.all_to_all(second, "ctx", split_axis=0, concat_axis=0, tiled=True)
    enter_here = back[:, :HEAD_DIM].reshape(GROUPS, HEADS // GROUPS, HEAD_DIM, STATE)
    halo_kv = back[:, HEAD_DIM:].reshape(devices * HALO * share, kv_cols)
    halo_pos = (
        (my_block - HALO + jnp.arange(HALO))[None, :, None] * tok_rows
        + share * jnp.arange(devices)[:, None, None]
        + jnp.arange(share)[None, None, :]
    ).reshape(-1)

    reach = jnp.where((my_seg == my_prev)[:, None], jnp.exp(cum_log), 0.0)
    read_out = jnp.einsum(
        "tgs,gkps->tgkp", readout, enter_here, preferred_element_type=jnp.float32
    ).reshape(tok_rows, HEADS, HEAD_DIM)
    outputs = local_out + read_out * reach[..., None] + skip_gain[0][:, None] * values
    mamba_out = outputs.astype(jnp.bfloat16).reshape(tok_rows, HEADS * HEAD_DIM)
    residual = inputs.astype(jnp.float32) + group_norm(mamba_out.astype(jnp.float32), mamba_gain[0])
    hidden = residual.astype(jnp.bfloat16)

    repeat = QHEADS // KVHEADS
    all_kv = jnp.concatenate([halo_kv, kv], axis=0).reshape(-1, 2, KVHEADS, QDIM)
    keys = all_kv[:, 0]
    vals = all_kv[:, 1]
    key_pos = jnp.concatenate(
        [halo_pos, my_block * tok_rows + jnp.arange(tok_rows, dtype=jnp.int32)]
    )
    key_seg = jnp.take(segment, jnp.maximum(key_pos, 0))
    score_scale = 1.0 / math.sqrt(QDIM)
    pieces = 4
    rows = tok_rows // pieces
    handed = []
    for piece in range(pieces):
        part = slice(piece * rows, (piece + 1) * rows)
        hidden_part = hidden[part]
        if handed:
            hidden_part, _ = lax.optimization_barrier((hidden_part, result))
        queries = hidden_part.reshape(rows, KVHEADS, repeat, QDIM)
        query_pos = my_block * tok_rows + piece * rows + jnp.arange(rows, dtype=jnp.int32)
        allowed = (
            (my_seg[part][:, None] == key_seg[None, :])
            & (key_pos[None, :] <= query_pos[:, None])
            & (key_pos[None, :] >= 0)
        )
        logits = (
            jnp.einsum("tgrd,kgd->grtk", queries, keys, preferred_element_type=jnp.float32)
            * score_scale
        )
        logits = jnp.where(allowed, logits, -1e30)
        best = jnp.max(logits, axis=-1, keepdims=True)
        weights = jnp.exp(logits - best)
        total_weight = jnp.sum(weights, axis=-1)
        blended = jnp.einsum(
            "grtk,kgd->grtd", weights.astype(jnp.bfloat16), vals, preferred_element_type=jnp.float32
        )
        attended = (
            (blended / total_weight[..., None]).transpose(2, 0, 1, 3).reshape(rows, QHEADS * QDIM)
        )
        normed = (
            attended
            * lax.rsqrt(jnp.mean(attended * attended, axis=-1, keepdims=True) + epsilon)
            * attn_gain[0]
        )
        result = (hidden_part.astype(jnp.float32) + normed).astype(jnp.bfloat16)
        handed.append(passed_along(result[None], "phase", 1))
    return jnp.concatenate(handed, axis=1)


def solution(mesh):
    in_specs = (
        P("phase", "ctx", None),
        P("phase", "ctx", None),
        P("phase", "ctx", None),
        P("phase", None),
        P("phase", None),
        P("phase", None),
        P("phase", None),
        P("phase", "ctx", None),
        P("phase", None),
        P("phase", None),
        P(),
    )
    out_specs = P("phase", "ctx", None)
    return jax.shard_map(
        on_device, mesh=mesh, in_specs=in_specs, out_specs=out_specs, check_vma=False
    )
```

```python
import math

import jax
import jax.numpy as jnp
from jax import lax
from jax.sharding import PartitionSpec as P

HEADS = 64
HEAD_DIM = 64
GROUPS = 8
STATE = 128
QHEADS = 32
KVHEADS = 2
QDIM = 128
HALO = 4


precise = lax.Precision.HIGHEST
epsilon = 1e-05


def passed_along(value, axis, steps):
    count = lax.axis_size(axis)
    pairs = [(source, (source + steps) % count) for source in range(count)]
    return lax.ppermute(value, axis, pairs)


def group_norm(values, gain):
    grouped = values.reshape(values.shape[0], GROUPS, -1)
    normed = grouped * lax.rsqrt(jnp.mean(grouped * grouped, axis=-1, keepdims=True) + epsilon)
    return normed.reshape(values.shape) * gain


def block_terms(values, inject, readout, step_sizes, rates, seg):
    length = values.shape[0]
    within = HEADS // GROUPS
    cum_log = jnp.cumsum(-rates * step_sizes, axis=0)
    positions = jnp.arange(length)
    allowed = (positions[:, None] >= positions[None, :]) & (seg[:, None] == seg[None, :])
    spread = cum_log.T[:, :, None] - cum_log.T[:, None, :]
    decays = jnp.where(allowed[None], jnp.exp(jnp.minimum(spread, 0.0)), 0.0)
    scores = jnp.einsum("tgs,ugs->gtu", readout, inject, preferred_element_type=jnp.float32)
    weights = decays.reshape(GROUPS, within, length, length) * scores[:, None]
    scaled = values * step_sizes[..., None]
    local_out = jnp.einsum(
        "gktu,ugkp->tgkp",
        weights,
        scaled.reshape(length, GROUPS, within, HEAD_DIM),
        precision=precise,
    ).reshape(values.shape)
    ending = cum_log[-1]
    to_end = jnp.where((seg == seg[-1])[:, None], jnp.exp(ending[None, :] - cum_log), 0.0)
    weighted = (scaled * to_end[..., None]).reshape(length, GROUPS, within, HEAD_DIM)
    states = jnp.einsum(
        "tgkp,tgs->gkps", weighted, inject.astype(jnp.float32), precision=precise
    ).reshape(HEADS, HEAD_DIM, STATE)
    return local_out, states, cum_log, ending


def on_device(
    mixer_input,
    state_proj,
    dt_raw,
    decay_rate,
    dt_bias,
    skip_gain,
    mamba_gain,
    keys_values,
    attn_gain,
    documents,
    placement_perm,
):
    devices = lax.axis_size("ctx")
    myself = lax.axis_index("ctx")
    tok_rows = mixer_input.shape[1]
    kv_cols = keys_values.shape[2]
    slice_cols = kv_cols // devices
    inverse = (
        jnp.zeros((devices,), jnp.int32)
        .at[placement_perm]
        .set(jnp.arange(devices, dtype=jnp.int32))
    )
    segment = documents[0]
    block_seg = segment.reshape(devices, tok_rows)
    seg_end = block_seg[:, -1]
    seg_prev = jnp.concatenate([jnp.full((1,), -1, jnp.int32), seg_end[:-1]])
    my_block = placement_perm[myself]
    my_seg = lax.dynamic_slice_in_dim(segment, my_block * tok_rows, tok_rows, 0)
    my_prev = seg_prev[my_block]

    inputs = mixer_input[0]
    values = inputs.astype(jnp.float32).reshape(tok_rows, HEADS, HEAD_DIM)
    paired = state_proj[0].reshape(tok_rows, GROUPS, 2, STATE)
    inject = paired[:, :, 0]
    readout = paired[:, :, 1]
    step_sizes = jax.nn.softplus(dt_raw[0].astype(jnp.float32) + dt_bias[0])
    local_out, states, cum_log, ending = block_terms(
        values, inject, readout, step_sizes, decay_rate[0], my_seg
    )

    kv = keys_values[0]
    lanes = 128
    share = tok_rows // devices
    kv_rows = share * kv_cols // lanes
    kv_slices = kv.reshape(devices, kv_rows, lanes)
    raw_cols = dt_raw[0].T.reshape(HEADS, 1, tok_rows)
    state_slots = states.astype(jnp.bfloat16)
    used = HEAD_DIM + kv_rows + 1
    padding = jnp.zeros((devices, -used % 8, lanes), jnp.bfloat16)
    first = jnp.concatenate([state_slots, kv_slices, raw_cols, padding], axis=1)
    got = lax.all_to_all(first, "ctx", split_axis=0, concat_axis=0, tiled=True)
    got_kv = got[:, HEAD_DIM : HEAD_DIM + kv_rows]
    got_raw = got[:, HEAD_DIM + kv_rows].astype(jnp.float32)

    my_rate = decay_rate[0][myself]
    my_bias = dt_bias[0][myself]
    my_steps = jax.nn.softplus(got_raw + my_bias)
    endings = jnp.cumsum(-my_rate * my_steps, axis=1)[:, -1]
    ending_pos = endings[inverse]
    running = jnp.cumsum(ending_pos)
    before = running - ending_pos
    positions = jnp.arange(devices)
    linked = (positions[None, :] < positions[:, None]) & (seg_end[None, :] == seg_prev[:, None])
    factors = jnp.where(
        linked, jnp.exp(jnp.minimum(before[:, None] - running[None, :], 0.0)), 0.0
    )
    by_device = factors[placement_perm][:, placement_perm]
    flat_states = got[:, :HEAD_DIM].reshape(devices, HEAD_DIM * STATE)
    high = by_device.astype(jnp.bfloat16)
    low = (by_device - high.astype(jnp.float32)).astype(jnp.bfloat16)
    entering = jnp.dot(high, flat_states, preferred_element_type=jnp.float32) + jnp.dot(
        low, flat_states, preferred_element_type=jnp.float32
    )
    entering = entering.reshape(devices, HEAD_DIM, STATE)

    halo_blocks = placement_perm[:, None] - HALO + jnp.arange(HALO)[None, :]
    halo_src = inverse[jnp.clip(halo_blocks, 0, devices - 1)]
    halo = got_kv[halo_src].reshape(devices, HALO * kv_rows, lanes)
    second = jnp.concatenate([entering.astype(jnp.bfloat16), halo], axis=1)
    back = lax.all_to_all(second, "ctx", split_axis=0, concat_axis=0, tiled=True)
    enter_here = back[:, :HEAD_DIM].reshape(GROUPS, HEADS // GROUPS, HEAD_DIM, STATE)
    halo_kv = back[:, HEAD_DIM:].reshape(devices * HALO * share, kv_cols)
    halo_pos = (
        (my_block - HALO + jnp.arange(HALO))[None, :, None] * tok_rows
        + share * jnp.arange(devices)[:, None, None]
        + jnp.arange(share)[None, None, :]
    ).reshape(-1)

    reach = jnp.where((my_seg == my_prev)[:, None], jnp.exp(cum_log), 0.0)
    read_out = jnp.einsum(
        "tgs,gkps->tgkp", readout, enter_here, preferred_element_type=jnp.float32
    ).reshape(tok_rows, HEADS, HEAD_DIM)
    outputs = local_out + read_out * reach[..., None] + skip_gain[0][:, None] * values
    mamba_out = outputs.astype(jnp.bfloat16).reshape(tok_rows, HEADS * HEAD_DIM)
    residual = inputs.astype(jnp.float32) + group_norm(mamba_out.astype(jnp.float32), mamba_gain[0])
    hidden = residual.astype(jnp.bfloat16)

    repeat = QHEADS // KVHEADS
    all_kv = jnp.concatenate([halo_kv, kv], axis=0).reshape(-1, 2, KVHEADS, QDIM)
    keys = all_kv[:, 0]
    vals = all_kv[:, 1]
    key_pos = jnp.concatenate(
        [halo_pos, my_block * tok_rows + jnp.arange(tok_rows, dtype=jnp.int32)]
    )
    key_seg = jnp.take(segment, jnp.maximum(key_pos, 0))
    score_scale = 1.0 / math.sqrt(QDIM)
    pieces = 2
    rows = tok_rows // pieces
    handed = []
    for piece in range(pieces):
        part = slice(piece * rows, (piece + 1) * rows)
        hidden_part = hidden[part]
        if handed:
            hidden_part, _ = lax.optimization_barrier((hidden_part, result))
        queries = hidden_part.reshape(rows, KVHEADS, repeat, QDIM)
        query_pos = my_block * tok_rows + piece * rows + jnp.arange(rows, dtype=jnp.int32)
        allowed = (
            (my_seg[part][:, None] == key_seg[None, :])
            & (key_pos[None, :] <= query_pos[:, None])
            & (key_pos[None, :] >= 0)
        )
        logits = (
            jnp.einsum("tgrd,kgd->grtk", queries, keys, preferred_element_type=jnp.float32)
            * score_scale
        )
        logits = jnp.where(allowed, logits, -1e30)
        best = jnp.max(logits, axis=-1, keepdims=True)
        weights = jnp.exp(logits - best)
        total_weight = jnp.sum(weights, axis=-1)
        blended = jnp.einsum(
            "grtk,kgd->grtd", weights.astype(jnp.bfloat16), vals, preferred_element_type=jnp.float32
        )
        attended = (
            (blended / total_weight[..., None]).transpose(2, 0, 1, 3).reshape(rows, QHEADS * QDIM)
        )
        normed = (
            attended
            * lax.rsqrt(jnp.mean(attended * attended, axis=-1, keepdims=True) + epsilon)
            * attn_gain[0]
        )
        result = (hidden_part.astype(jnp.float32) + normed).astype(jnp.bfloat16)
        handed.append(passed_along(result[None], "phase", 1))
    return jnp.concatenate(handed, axis=1)


def solution(mesh):
    in_specs = (
        P("phase", "ctx", None),
        P("phase", "ctx", None),
        P("phase", "ctx", None),
        P("phase", None),
        P("phase", None),
        P("phase", None),
        P("phase", None),
        P("phase", "ctx", None),
        P("phase", None),
        P("phase", None),
        P(),
    )
    out_specs = P("phase", "ctx", None)
    return jax.shard_map(
        on_device, mesh=mesh, in_specs=in_specs, out_specs=out_specs, check_vma=False
    )
```

```python
import math

import jax
import jax.numpy as jnp
from jax import lax
from jax.experimental import pallas as pl
from jax.experimental.pallas import tpu as pltpu
from jax.sharding import PartitionSpec as P

HEADS = 64
HEAD_DIM = 64
GROUPS = 8
STATE = 128
QHEADS = 32
KVHEADS = 2
QDIM = 128
HALO = 4


precise = lax.Precision.HIGHEST
epsilon = 1e-05


def passed_along(value, axis, steps):
    count = lax.axis_size(axis)
    pairs = [(source, (source + steps) % count) for source in range(count)]
    return lax.ppermute(value, axis, pairs)


def group_norm(values, gain):
    grouped = values.reshape(values.shape[0], GROUPS, -1)
    normed = grouped * lax.rsqrt(jnp.mean(grouped * grouped, axis=-1, keepdims=True) + epsilon)
    return normed.reshape(values.shape) * gain


def block_terms(values, inject, readout, step_sizes, rates, seg):
    length = values.shape[0]
    within = HEADS // GROUPS
    cum_log = jnp.cumsum(-rates * step_sizes, axis=0)
    positions = jnp.arange(length)
    allowed = (positions[:, None] >= positions[None, :]) & (seg[:, None] == seg[None, :])
    spread = cum_log.T[:, :, None] - cum_log.T[:, None, :]
    decays = jnp.where(allowed[None], jnp.exp(jnp.minimum(spread, 0.0)), 0.0)
    scores = jnp.einsum("tgs,ugs->gtu", readout, inject, preferred_element_type=jnp.float32)
    weights = decays.reshape(GROUPS, within, length, length) * scores[:, None]
    scaled = values * step_sizes[..., None]
    local_out = jnp.einsum(
        "gktu,ugkp->tgkp",
        weights,
        scaled.reshape(length, GROUPS, within, HEAD_DIM),
        precision=precise,
    ).reshape(values.shape)
    ending = cum_log[-1]
    to_end = jnp.where((seg == seg[-1])[:, None], jnp.exp(ending[None, :] - cum_log), 0.0)
    weighted = (scaled * to_end[..., None]).reshape(length, GROUPS, within, HEAD_DIM)
    states = jnp.einsum(
        "tgkp,tgs->gkps", weighted, inject.astype(jnp.float32), precision=precise
    ).reshape(HEADS, HEAD_DIM, STATE)
    return local_out, states, cum_log, ending


def states_kernel(xt_ref, bc_ref, raw_ref, bias_ref, rate_ref, seg_ref, tail_ref, out_ref, cum_ref):
    length = raw_ref.shape[1]
    within = HEADS // GROUPS
    shifted = raw_ref[...].astype(jnp.float32) + bias_ref[...]
    steps = jnp.maximum(shifted, 0.0) + jnp.log1p(jnp.exp(-jnp.abs(shifted)))
    cum = -rate_ref[...] * steps
    lane = lax.broadcasted_iota(jnp.int32, cum.shape, 1)
    reach = 1
    while reach < length:
        cum = cum + jnp.where(lane >= reach, pltpu.roll(cum, reach, 1), 0.0)
        reach *= 2
    cum_ref[...] = cum
    ending = cum[:, length - 1 : length]
    seg = seg_ref[...]
    same = seg == seg[:, length - 1 : length]
    weights = jnp.where(same, jnp.exp(ending - cum), 0.0) * steps
    for group in range(GROUPS):
        w = weights[group * within : (group + 1) * within]
        w = jnp.broadcast_to(w[:, None, :], (within, HEAD_DIM, length)).reshape(within * HEAD_DIM, length)
        rows = slice(group * within * HEAD_DIM, (group + 1) * within * HEAD_DIM)
        scaled = xt_ref[rows, :].astype(jnp.float32) * w
        high = scaled.astype(jnp.bfloat16)
        low = (scaled - high.astype(jnp.float32)).astype(jnp.bfloat16)
        inject = bc_ref[:, group * 2 * STATE : group * 2 * STATE + STATE]
        state = jnp.dot(high, inject, preferred_element_type=jnp.float32) + jnp.dot(
            low, inject, preferred_element_type=jnp.float32
        )
        out_ref[group * within : (group + 1) * within, :HEAD_DIM, :] = (
            state.astype(out_ref.dtype).reshape(within, HEAD_DIM, STATE)
        )
    out_ref[:, HEAD_DIM:, :] = tail_ref[...]


def block_states(inputs, projections, raw, bias, rate, seg, tail):
    tokens = inputs.shape[0]
    rows = HEAD_DIM + tail.shape[1]
    return pl.pallas_call(
        states_kernel,
        out_shape=(
            jax.ShapeDtypeStruct((HEADS, rows, STATE), jnp.bfloat16),
            jax.ShapeDtypeStruct((HEADS, tokens), jnp.float32),
        ),
        cost_estimate=pl.CostEstimate(
            flops=4 * HEADS * HEAD_DIM * STATE * tokens,
            transcendentals=3 * HEADS * tokens,
            bytes_accessed=inputs.size * 2 + projections.size * 2 + HEADS * rows * STATE * 2,
        ),
    )(
        inputs.T,
        projections,
        raw.T,
        bias.reshape(HEADS, 1),
        rate.reshape(HEADS, 1),
        seg.reshape(1, tokens),
        tail,
    )


def on_device(
    mixer_input,
    state_proj,
    dt_raw,
    decay_rate,
    dt_bias,
    skip_gain,
    mamba_gain,
    keys_values,
    attn_gain,
    documents,
    placement_perm,
):
    devices = lax.axis_size("ctx")
    myself = lax.axis_index("ctx")
    tok_rows = mixer_input.shape[1]
    kv_cols = keys_values.shape[2]
    slice_cols = kv_cols // devices
    inverse = (
        jnp.zeros((devices,), jnp.int32)
        .at[placement_perm]
        .set(jnp.arange(devices, dtype=jnp.int32))
    )
    segment = documents[0]
    block_seg = segment.reshape(devices, tok_rows)
    seg_end = block_seg[:, -1]
    seg_prev = jnp.concatenate([jnp.full((1,), -1, jnp.int32), seg_end[:-1]])
    my_block = placement_perm[myself]
    my_seg = lax.dynamic_slice_in_dim(segment, my_block * tok_rows, tok_rows, 0)
    my_prev = seg_prev[my_block]

    inputs = mixer_input[0]
    values = inputs.astype(jnp.float32).reshape(tok_rows, HEADS, HEAD_DIM)
    paired = state_proj[0].reshape(tok_rows, GROUPS, 2, STATE)
    inject = paired[:, :, 0]
    readout = paired[:, :, 1]
    step_sizes = jax.nn.softplus(dt_raw[0].astype(jnp.float32) + dt_bias[0])
    local_out, states, cum_log, ending = block_terms(
        values, inject, readout, step_sizes, decay_rate[0], my_seg
    )

    kv = keys_values[0]
    lanes = 128
    share = tok_rows // devices
    kv_rows = share * kv_cols // lanes
    kv_slices = kv.reshape(devices, kv_rows, lanes)
    raw_cols = dt_raw[0].T.reshape(HEADS, 1, tok_rows)
    used = kv_rows + 1
    padding = jnp.zeros((devices, -used % 8, lanes), jnp.bfloat16)
    tail = jnp.concatenate([kv_slices, raw_cols, padding], axis=1)
    first, cum_t = block_states(
        inputs, state_proj[0], dt_raw[0], dt_bias[0], decay_rate[0], my_seg, tail
    )
    cum_log = cum_t.T
    got = lax.all_to_all(first, "ctx", split_axis=0, concat_axis=0, tiled=True)
    got_kv = got[:, HEAD_DIM : HEAD_DIM + kv_rows]
    got_raw = got[:, HEAD_DIM + kv_rows].astype(jnp.float32)

    my_rate = decay_rate[0][myself]
    my_bias = dt_bias[0][myself]
    my_steps = jax.nn.softplus(got_raw + my_bias)
    endings = jnp.cumsum(-my_rate * my_steps, axis=1)[:, -1]
    ending_pos = endings[inverse]
    running = jnp.cumsum(ending_pos)
    before = running - ending_pos
    positions = jnp.arange(devices)
    linked = (positions[None, :] < positions[:, None]) & (seg_end[None, :] == seg_prev[:, None])
    factors = jnp.where(
        linked, jnp.exp(jnp.minimum(before[:, None] - running[None, :], 0.0)), 0.0
    )
    by_device = factors[placement_perm][:, placement_perm]
    flat_states = got[:, :HEAD_DIM].reshape(devices, HEAD_DIM * STATE)
    high = by_device.astype(jnp.bfloat16)
    low = (by_device - high.astype(jnp.float32)).astype(jnp.bfloat16)
    entering = jnp.dot(high, flat_states, preferred_element_type=jnp.float32) + jnp.dot(
        low, flat_states, preferred_element_type=jnp.float32
    )
    entering = entering.reshape(devices, HEAD_DIM, STATE)

    halo_blocks = placement_perm[:, None] - HALO + jnp.arange(HALO)[None, :]
    halo_src = inverse[jnp.clip(halo_blocks, 0, devices - 1)]
    halo = got_kv[halo_src].reshape(devices, HALO * kv_rows, lanes)
    second = jnp.concatenate([entering.astype(jnp.bfloat16), halo], axis=1)
    back = lax.all_to_all(second, "ctx", split_axis=0, concat_axis=0, tiled=True)
    enter_here = back[:, :HEAD_DIM].reshape(GROUPS, HEADS // GROUPS, HEAD_DIM, STATE)
    halo_kv = back[:, HEAD_DIM:].reshape(devices * HALO * share, kv_cols)
    halo_pos = (
        (my_block - HALO + jnp.arange(HALO))[None, :, None] * tok_rows
        + share * jnp.arange(devices)[:, None, None]
        + jnp.arange(share)[None, None, :]
    ).reshape(-1)

    reach = jnp.where((my_seg == my_prev)[:, None], jnp.exp(cum_log), 0.0)
    read_out = jnp.einsum(
        "tgs,gkps->tgkp", readout, enter_here, preferred_element_type=jnp.float32
    ).reshape(tok_rows, HEADS, HEAD_DIM)
    outputs = local_out + read_out * reach[..., None] + skip_gain[0][:, None] * values
    mamba_out = outputs.astype(jnp.bfloat16).reshape(tok_rows, HEADS * HEAD_DIM)
    residual = inputs.astype(jnp.float32) + group_norm(mamba_out.astype(jnp.float32), mamba_gain[0])
    hidden = residual.astype(jnp.bfloat16)

    repeat = QHEADS // KVHEADS
    all_kv = jnp.concatenate([halo_kv, kv], axis=0).reshape(-1, 2, KVHEADS, QDIM)
    keys = all_kv[:, 0]
    vals = all_kv[:, 1]
    key_pos = jnp.concatenate(
        [halo_pos, my_block * tok_rows + jnp.arange(tok_rows, dtype=jnp.int32)]
    )
    key_seg = jnp.take(segment, jnp.maximum(key_pos, 0))
    score_scale = 1.0 / math.sqrt(QDIM)
    pieces = 2
    rows = tok_rows // pieces
    handed = []
    for piece in range(pieces):
        part = slice(piece * rows, (piece + 1) * rows)
        hidden_part = hidden[part]
        if handed:
            hidden_part, _ = lax.optimization_barrier((hidden_part, result))
        queries = hidden_part.reshape(rows, KVHEADS, repeat, QDIM)
        query_pos = my_block * tok_rows + piece * rows + jnp.arange(rows, dtype=jnp.int32)
        allowed = (
            (my_seg[part][:, None] == key_seg[None, :])
            & (key_pos[None, :] <= query_pos[:, None])
            & (key_pos[None, :] >= 0)
        )
        logits = (
            jnp.einsum("tgrd,kgd->grtk", queries, keys, preferred_element_type=jnp.float32)
            * score_scale
        )
        logits = jnp.where(allowed, logits, -1e30)
        best = jnp.max(logits, axis=-1, keepdims=True)
        weights = jnp.exp(logits - best)
        total_weight = jnp.sum(weights, axis=-1)
        blended = jnp.einsum(
            "grtk,kgd->grtd", weights.astype(jnp.bfloat16), vals, preferred_element_type=jnp.float32
        )
        attended = (
            (blended / total_weight[..., None]).transpose(2, 0, 1, 3).reshape(rows, QHEADS * QDIM)
        )
        normed = (
            attended
            * lax.rsqrt(jnp.mean(attended * attended, axis=-1, keepdims=True) + epsilon)
            * attn_gain[0]
        )
        result = (hidden_part.astype(jnp.float32) + normed).astype(jnp.bfloat16)
        handed.append(passed_along(result[None], "phase", 1))
    return jnp.concatenate(handed, axis=1)


def solution(mesh):
    in_specs = (
        P("phase", "ctx", None),
        P("phase", "ctx", None),
        P("phase", "ctx", None),
        P("phase", None),
        P("phase", None),
        P("phase", None),
        P("phase", None),
        P("phase", "ctx", None),
        P("phase", None),
        P("phase", None),
        P(),
    )
    out_specs = P("phase", "ctx", None)
    return jax.shard_map(
        on_device, mesh=mesh, in_specs=in_specs, out_specs=out_specs, check_vma=False
    )
```

```python
import math

import jax
import jax.numpy as jnp
from jax import lax
from jax.experimental import pallas as pl
from jax.experimental.pallas import tpu as pltpu
from jax.sharding import PartitionSpec as P

HEADS = 64
HEAD_DIM = 64
GROUPS = 8
STATE = 128
QHEADS = 32
KVHEADS = 2
QDIM = 128
HALO = 4


precise = lax.Precision.HIGHEST
epsilon = 1e-05


def passed_along(value, axis, steps):
    count = lax.axis_size(axis)
    pairs = [(source, (source + steps) % count) for source in range(count)]
    return lax.ppermute(value, axis, pairs)


def group_norm(values, gain):
    grouped = values.reshape(values.shape[0], GROUPS, -1)
    normed = grouped * lax.rsqrt(jnp.mean(grouped * grouped, axis=-1, keepdims=True) + epsilon)
    return normed.reshape(values.shape) * gain


def block_terms(values, inject, readout, step_sizes, rates, seg):
    length = values.shape[0]
    within = HEADS // GROUPS
    cum_log = jnp.cumsum(-rates * step_sizes, axis=0)
    positions = jnp.arange(length)
    allowed = (positions[:, None] >= positions[None, :]) & (seg[:, None] == seg[None, :])
    spread = cum_log.T[:, :, None] - cum_log.T[:, None, :]
    decays = jnp.where(allowed[None], jnp.exp(jnp.minimum(spread, 0.0)), 0.0)
    scores = jnp.einsum("tgs,ugs->gtu", readout, inject, preferred_element_type=jnp.float32)
    weights = decays.reshape(GROUPS, within, length, length) * scores[:, None]
    scaled = values * step_sizes[..., None]
    local_out = jnp.einsum(
        "gktu,ugkp->tgkp",
        weights,
        scaled.reshape(length, GROUPS, within, HEAD_DIM),
        precision=precise,
    ).reshape(values.shape)
    ending = cum_log[-1]
    to_end = jnp.where((seg == seg[-1])[:, None], jnp.exp(ending[None, :] - cum_log), 0.0)
    weighted = (scaled * to_end[..., None]).reshape(length, GROUPS, within, HEAD_DIM)
    states = jnp.einsum(
        "tgkp,tgs->gkps", weighted, inject.astype(jnp.float32), precision=precise
    ).reshape(HEADS, HEAD_DIM, STATE)
    return local_out, states, cum_log, ending


def states_kernel(xt_ref, bc_ref, raw_ref, bias_ref, rate_ref, seg_ref, tail_ref, out_ref, cum_ref):
    length = raw_ref.shape[0]
    within = HEADS // GROUPS
    shifted = raw_ref[...].astype(jnp.float32) + bias_ref[...]
    steps = jnp.maximum(shifted, 0.0) + jnp.log1p(jnp.exp(-jnp.abs(shifted)))
    cum = -rate_ref[...] * steps
    row = lax.broadcasted_iota(jnp.int32, cum.shape, 0)
    reach = 1
    while reach < length:
        cum = cum + jnp.where(row >= reach, pltpu.roll(cum, reach, 0), 0.0)
        reach *= 2
    cum_ref[...] = cum
    ending = cum[length - 1 : length, :]
    seg = seg_ref[...]
    same = seg == seg[length - 1 : length, :]
    weights = (jnp.where(same, jnp.exp(ending - cum), 0.0) * steps).T
    for group in range(GROUPS):
        w = weights[group * within : (group + 1) * within]
        w = jnp.broadcast_to(w[:, None, :], (within, HEAD_DIM, length)).reshape(within * HEAD_DIM, length)
        rows = slice(group * within * HEAD_DIM, (group + 1) * within * HEAD_DIM)
        scaled = xt_ref[rows, :].astype(jnp.float32) * w
        high = scaled.astype(jnp.bfloat16)
        low = (scaled - high.astype(jnp.float32)).astype(jnp.bfloat16)
        inject = bc_ref[:, group * 2 * STATE : group * 2 * STATE + STATE]
        state = jnp.dot(high, inject, preferred_element_type=jnp.float32) + jnp.dot(
            low, inject, preferred_element_type=jnp.float32
        )
        out_ref[group * within : (group + 1) * within, :HEAD_DIM, :] = (
            state.astype(out_ref.dtype).reshape(within, HEAD_DIM, STATE)
        )
    out_ref[:, HEAD_DIM:, :] = tail_ref[...]


def block_states(inputs, projections, raw, bias, rate, seg, tail):
    tokens = inputs.shape[0]
    rows = HEAD_DIM + tail.shape[1]
    return pl.pallas_call(
        states_kernel,
        out_shape=(
            jax.ShapeDtypeStruct((HEADS, rows, STATE), jnp.bfloat16),
            jax.ShapeDtypeStruct((tokens, HEADS), jnp.float32),
        ),
        cost_estimate=pl.CostEstimate(
            flops=4 * HEADS * HEAD_DIM * STATE * tokens,
            transcendentals=3 * HEADS * tokens,
            bytes_accessed=inputs.size * 2 + projections.size * 2 + HEADS * rows * STATE * 2,
        ),
    )(
        inputs.T,
        projections,
        raw,
        bias.reshape(1, HEADS),
        rate.reshape(1, HEADS),
        seg.reshape(tokens, 1),
        tail,
    )


def on_device(
    mixer_input,
    state_proj,
    dt_raw,
    decay_rate,
    dt_bias,
    skip_gain,
    mamba_gain,
    keys_values,
    attn_gain,
    documents,
    placement_perm,
):
    devices = lax.axis_size("ctx")
    myself = lax.axis_index("ctx")
    tok_rows = mixer_input.shape[1]
    kv_cols = keys_values.shape[2]
    slice_cols = kv_cols // devices
    inverse = (
        jnp.zeros((devices,), jnp.int32)
        .at[placement_perm]
        .set(jnp.arange(devices, dtype=jnp.int32))
    )
    segment = documents[0]
    block_seg = segment.reshape(devices, tok_rows)
    seg_end = block_seg[:, -1]
    seg_prev = jnp.concatenate([jnp.full((1,), -1, jnp.int32), seg_end[:-1]])
    my_block = placement_perm[myself]
    my_seg = lax.dynamic_slice_in_dim(segment, my_block * tok_rows, tok_rows, 0)
    my_prev = seg_prev[my_block]

    inputs = mixer_input[0]
    values = inputs.astype(jnp.float32).reshape(tok_rows, HEADS, HEAD_DIM)
    paired = state_proj[0].reshape(tok_rows, GROUPS, 2, STATE)
    inject = paired[:, :, 0]
    readout = paired[:, :, 1]
    step_sizes = jax.nn.softplus(dt_raw[0].astype(jnp.float32) + dt_bias[0])
    local_out, states, cum_log, ending = block_terms(
        values, inject, readout, step_sizes, decay_rate[0], my_seg
    )

    kv = keys_values[0]
    lanes = 128
    share = tok_rows // devices
    kv_rows = share * kv_cols // lanes
    kv_slices = kv.reshape(devices, kv_rows, lanes)
    raw_cols = dt_raw[0].T.reshape(HEADS, 1, tok_rows)
    used = kv_rows + 1
    padding = jnp.zeros((devices, -used % 8, lanes), jnp.bfloat16)
    tail = jnp.concatenate([kv_slices, raw_cols, padding], axis=1)
    first, cum_log = block_states(
        inputs, state_proj[0], dt_raw[0], dt_bias[0], decay_rate[0], my_seg, tail
    )
    got = lax.all_to_all(first, "ctx", split_axis=0, concat_axis=0, tiled=True)
    got_kv = got[:, HEAD_DIM : HEAD_DIM + kv_rows]
    got_raw = got[:, HEAD_DIM + kv_rows].astype(jnp.float32)

    my_rate = decay_rate[0][myself]
    my_bias = dt_bias[0][myself]
    my_steps = jax.nn.softplus(got_raw + my_bias)
    endings = jnp.cumsum(-my_rate * my_steps, axis=1)[:, -1]
    ending_pos = endings[inverse]
    running = jnp.cumsum(ending_pos)
    before = running - ending_pos
    positions = jnp.arange(devices)
    linked = (positions[None, :] < positions[:, None]) & (seg_end[None, :] == seg_prev[:, None])
    factors = jnp.where(
        linked, jnp.exp(jnp.minimum(before[:, None] - running[None, :], 0.0)), 0.0
    )
    by_device = factors[placement_perm][:, placement_perm]
    flat_states = got[:, :HEAD_DIM].reshape(devices, HEAD_DIM * STATE)
    high = by_device.astype(jnp.bfloat16)
    low = (by_device - high.astype(jnp.float32)).astype(jnp.bfloat16)
    entering = jnp.dot(high, flat_states, preferred_element_type=jnp.float32) + jnp.dot(
        low, flat_states, preferred_element_type=jnp.float32
    )
    entering = entering.reshape(devices, HEAD_DIM, STATE)

    halo_blocks = placement_perm[:, None] - HALO + jnp.arange(HALO)[None, :]
    halo_src = inverse[jnp.clip(halo_blocks, 0, devices - 1)]
    halo = got_kv[halo_src].reshape(devices, HALO * kv_rows, lanes)
    second = jnp.concatenate([entering.astype(jnp.bfloat16), halo], axis=1)
    back = lax.all_to_all(second, "ctx", split_axis=0, concat_axis=0, tiled=True)
    enter_here = back[:, :HEAD_DIM].reshape(GROUPS, HEADS // GROUPS, HEAD_DIM, STATE)
    halo_kv = back[:, HEAD_DIM:].reshape(devices * HALO * share, kv_cols)
    halo_pos = (
        (my_block - HALO + jnp.arange(HALO))[None, :, None] * tok_rows
        + share * jnp.arange(devices)[:, None, None]
        + jnp.arange(share)[None, None, :]
    ).reshape(-1)

    reach = jnp.where((my_seg == my_prev)[:, None], jnp.exp(cum_log), 0.0)
    read_out = jnp.einsum(
        "tgs,gkps->tgkp", readout, enter_here, preferred_element_type=jnp.float32
    ).reshape(tok_rows, HEADS, HEAD_DIM)
    outputs = local_out + read_out * reach[..., None] + skip_gain[0][:, None] * values
    mamba_out = outputs.astype(jnp.bfloat16).reshape(tok_rows, HEADS * HEAD_DIM)
    residual = inputs.astype(jnp.float32) + group_norm(mamba_out.astype(jnp.float32), mamba_gain[0])
    hidden = residual.astype(jnp.bfloat16)

    repeat = QHEADS // KVHEADS
    all_kv = jnp.concatenate([halo_kv, kv], axis=0).reshape(-1, 2, KVHEADS, QDIM)
    keys = all_kv[:, 0]
    vals = all_kv[:, 1]
    key_pos = jnp.concatenate(
        [halo_pos, my_block * tok_rows + jnp.arange(tok_rows, dtype=jnp.int32)]
    )
    key_seg = jnp.take(segment, jnp.maximum(key_pos, 0))
    score_scale = 1.0 / math.sqrt(QDIM)
    pieces = 2
    rows = tok_rows // pieces
    handed = []
    for piece in range(pieces):
        part = slice(piece * rows, (piece + 1) * rows)
        hidden_part = hidden[part]
        if handed:
            hidden_part, _ = lax.optimization_barrier((hidden_part, result))
        queries = hidden_part.reshape(rows, KVHEADS, repeat, QDIM)
        query_pos = my_block * tok_rows + piece * rows + jnp.arange(rows, dtype=jnp.int32)
        allowed = (
            (my_seg[part][:, None] == key_seg[None, :])
            & (key_pos[None, :] <= query_pos[:, None])
            & (key_pos[None, :] >= 0)
        )
        logits = (
            jnp.einsum("tgrd,kgd->grtk", queries, keys, preferred_element_type=jnp.float32)
            * score_scale
        )
        logits = jnp.where(allowed, logits, -1e30)
        best = jnp.max(logits, axis=-1, keepdims=True)
        weights = jnp.exp(logits - best)
        total_weight = jnp.sum(weights, axis=-1)
        blended = jnp.einsum(
            "grtk,kgd->grtd", weights.astype(jnp.bfloat16), vals, preferred_element_type=jnp.float32
        )
        attended = (
            (blended / total_weight[..., None]).transpose(2, 0, 1, 3).reshape(rows, QHEADS * QDIM)
        )
        normed = (
            attended
            * lax.rsqrt(jnp.mean(attended * attended, axis=-1, keepdims=True) + epsilon)
            * attn_gain[0]
        )
        result = (hidden_part.astype(jnp.float32) + normed).astype(jnp.bfloat16)
        handed.append(passed_along(result[None], "phase", 1))
    return jnp.concatenate(handed, axis=1)


def solution(mesh):
    in_specs = (
        P("phase", "ctx", None),
        P("phase", "ctx", None),
        P("phase", "ctx", None),
        P("phase", None),
        P("phase", None),
        P("phase", None),
        P("phase", None),
        P("phase", "ctx", None),
        P("phase", None),
        P("phase", None),
        P(),
    )
    out_specs = P("phase", "ctx", None)
    return jax.shard_map(
        on_device, mesh=mesh, in_specs=in_specs, out_specs=out_specs, check_vma=False
    )
```

```python
import math

import jax
import jax.numpy as jnp
from jax import lax
from jax.experimental import pallas as pl
from jax.experimental.pallas import tpu as pltpu
from jax.sharding import PartitionSpec as P

HEADS = 64
HEAD_DIM = 64
GROUPS = 8
STATE = 128
QHEADS = 32
KVHEADS = 2
QDIM = 128
HALO = 4


precise = lax.Precision.HIGHEST
epsilon = 1e-05


def passed_along(value, axis, steps):
    count = lax.axis_size(axis)
    pairs = [(source, (source + steps) % count) for source in range(count)]
    return lax.ppermute(value, axis, pairs)


def group_norm(values, gain):
    grouped = values.reshape(values.shape[0], GROUPS, -1)
    normed = grouped * lax.rsqrt(jnp.mean(grouped * grouped, axis=-1, keepdims=True) + epsilon)
    return normed.reshape(values.shape) * gain


def block_terms(values, inject, readout, step_sizes, rates, seg):
    length = values.shape[0]
    within = HEADS // GROUPS
    cum_log = jnp.cumsum(-rates * step_sizes, axis=0)
    positions = jnp.arange(length)
    allowed = (positions[:, None] >= positions[None, :]) & (seg[:, None] == seg[None, :])
    spread = cum_log.T[:, :, None] - cum_log.T[:, None, :]
    decays = jnp.where(allowed[None], jnp.exp(jnp.minimum(spread, 0.0)), 0.0)
    scores = jnp.einsum("tgs,ugs->gtu", readout, inject, preferred_element_type=jnp.float32)
    weights = decays.reshape(GROUPS, within, length, length) * scores[:, None]
    scaled = values * step_sizes[..., None]
    local_out = jnp.einsum(
        "gktu,ugkp->tgkp",
        weights,
        scaled.reshape(length, GROUPS, within, HEAD_DIM),
        precision=precise,
    ).reshape(values.shape)
    ending = cum_log[-1]
    to_end = jnp.where((seg == seg[-1])[:, None], jnp.exp(ending[None, :] - cum_log), 0.0)
    weighted = (scaled * to_end[..., None]).reshape(length, GROUPS, within, HEAD_DIM)
    states = jnp.einsum(
        "tgkp,tgs->gkps", weighted, inject.astype(jnp.float32), precision=precise
    ).reshape(HEADS, HEAD_DIM, STATE)
    return local_out, states, cum_log, ending


def states_kernel(x_ref, bc_ref, raw_ref, bias_ref, rate_ref, seg_ref, tail_ref, out_ref, cum_ref):
    length = raw_ref.shape[0]
    within = HEADS // GROUPS
    shifted = raw_ref[...].astype(jnp.float32) + bias_ref[...]
    steps = jnp.maximum(shifted, 0.0) + jnp.log1p(jnp.exp(-jnp.abs(shifted)))
    cum = -rate_ref[...] * steps
    row = lax.broadcasted_iota(jnp.int32, cum.shape, 0)
    reach = 1
    while reach < length:
        cum = cum + jnp.where(row >= reach, pltpu.roll(cum, reach, 0), 0.0)
        reach *= 2
    cum_ref[...] = cum
    ending = cum[length - 1 : length, :]
    seg = seg_ref[...]
    same = seg == seg[length - 1 : length, :]
    weights = jnp.where(same, jnp.exp(ending - cum), 0.0) * steps
    w_high = weights.astype(jnp.bfloat16)
    w_low = (weights - w_high.astype(jnp.float32)).astype(jnp.bfloat16)
    width = within * HEAD_DIM
    head_of = lax.broadcasted_iota(jnp.int32, (HEADS, width), 0)
    column = lax.broadcasted_iota(jnp.int32, (HEADS, width), 1)
    for group in range(GROUPS):
        spread = (column // HEAD_DIM + group * within == head_of).astype(jnp.bfloat16)
        w = jnp.dot(w_high, spread, preferred_element_type=jnp.float32) + jnp.dot(
            w_low, spread, preferred_element_type=jnp.float32
        )
        scaled = x_ref[:, group * width : (group + 1) * width].astype(jnp.float32) * w
        high = scaled.astype(jnp.bfloat16)
        low = (scaled - high.astype(jnp.float32)).astype(jnp.bfloat16)
        inject = bc_ref[:, group * 2 * STATE : group * 2 * STATE + STATE]
        over_tokens = (((0,), (0,)), ((), ()))
        state = lax.dot_general(
            high, inject, over_tokens, preferred_element_type=jnp.float32
        ) + lax.dot_general(low, inject, over_tokens, preferred_element_type=jnp.float32)
        out_ref[group * within : (group + 1) * within, :HEAD_DIM, :] = (
            state.astype(out_ref.dtype).reshape(within, HEAD_DIM, STATE)
        )
    out_ref[:, HEAD_DIM:, :] = tail_ref[...]


def block_states(inputs, projections, raw, bias, rate, seg, tail):
    tokens = inputs.shape[0]
    rows = HEAD_DIM + tail.shape[1]
    return pl.pallas_call(
        states_kernel,
        out_shape=(
            jax.ShapeDtypeStruct((HEADS, rows, STATE), jnp.bfloat16),
            jax.ShapeDtypeStruct((tokens, HEADS), jnp.float32),
        ),
        cost_estimate=pl.CostEstimate(
            flops=4 * HEADS * HEAD_DIM * STATE * tokens,
            transcendentals=3 * HEADS * tokens,
            bytes_accessed=inputs.size * 2 + projections.size * 2 + HEADS * rows * STATE * 2,
        ),
    )(
        inputs,
        projections,
        raw,
        bias.reshape(1, HEADS),
        rate.reshape(1, HEADS),
        seg.reshape(tokens, 1),
        tail,
    )


def on_device(
    mixer_input,
    state_proj,
    dt_raw,
    decay_rate,
    dt_bias,
    skip_gain,
    mamba_gain,
    keys_values,
    attn_gain,
    documents,
    placement_perm,
):
    devices = lax.axis_size("ctx")
    myself = lax.axis_index("ctx")
    tok_rows = mixer_input.shape[1]
    kv_cols = keys_values.shape[2]
    slice_cols = kv_cols // devices
    inverse = (
        jnp.zeros((devices,), jnp.int32)
        .at[placement_perm]
        .set(jnp.arange(devices, dtype=jnp.int32))
    )
    segment = documents[0]
    block_seg = segment.reshape(devices, tok_rows)
    seg_end = block_seg[:, -1]
    seg_prev = jnp.concatenate([jnp.full((1,), -1, jnp.int32), seg_end[:-1]])
    my_block = placement_perm[myself]
    my_seg = lax.dynamic_slice_in_dim(segment, my_block * tok_rows, tok_rows, 0)
    my_prev = seg_prev[my_block]

    inputs = mixer_input[0]
    values = inputs.astype(jnp.float32).reshape(tok_rows, HEADS, HEAD_DIM)
    paired = state_proj[0].reshape(tok_rows, GROUPS, 2, STATE)
    inject = paired[:, :, 0]
    readout = paired[:, :, 1]
    step_sizes = jax.nn.softplus(dt_raw[0].astype(jnp.float32) + dt_bias[0])
    local_out, states, cum_log, ending = block_terms(
        values, inject, readout, step_sizes, decay_rate[0], my_seg
    )

    kv = keys_values[0]
    lanes = 128
    share = tok_rows // devices
    kv_rows = share * kv_cols // lanes
    kv_slices = kv.reshape(devices, kv_rows, lanes)
    raw_cols = dt_raw[0].T.reshape(HEADS, 1, tok_rows)
    used = kv_rows + 1
    padding = jnp.zeros((devices, -used % 8, lanes), jnp.bfloat16)
    tail = jnp.concatenate([kv_slices, raw_cols, padding], axis=1)
    first, cum_log = block_states(
        inputs, state_proj[0], dt_raw[0], dt_bias[0], decay_rate[0], my_seg, tail
    )
    got = lax.all_to_all(first, "ctx", split_axis=0, concat_axis=0, tiled=True)
    got_kv = got[:, HEAD_DIM : HEAD_DIM + kv_rows]
    got_raw = got[:, HEAD_DIM + kv_rows].astype(jnp.float32)

    my_rate = decay_rate[0][myself]
    my_bias = dt_bias[0][myself]
    my_steps = jax.nn.softplus(got_raw + my_bias)
    endings = jnp.cumsum(-my_rate * my_steps, axis=1)[:, -1]
    ending_pos = endings[inverse]
    running = jnp.cumsum(ending_pos)
    before = running - ending_pos
    positions = jnp.arange(devices)
    linked = (positions[None, :] < positions[:, None]) & (seg_end[None, :] == seg_prev[:, None])
    factors = jnp.where(
        linked, jnp.exp(jnp.minimum(before[:, None] - running[None, :], 0.0)), 0.0
    )
    by_device = factors[placement_perm][:, placement_perm]
    flat_states = got[:, :HEAD_DIM].reshape(devices, HEAD_DIM * STATE)
    high = by_device.astype(jnp.bfloat16)
    low = (by_device - high.astype(jnp.float32)).astype(jnp.bfloat16)
    entering = jnp.dot(high, flat_states, preferred_element_type=jnp.float32) + jnp.dot(
        low, flat_states, preferred_element_type=jnp.float32
    )
    entering = entering.reshape(devices, HEAD_DIM, STATE)

    halo_blocks = placement_perm[:, None] - HALO + jnp.arange(HALO)[None, :]
    halo_src = inverse[jnp.clip(halo_blocks, 0, devices - 1)]
    halo = got_kv[halo_src].reshape(devices, HALO * kv_rows, lanes)
    second = jnp.concatenate([entering.astype(jnp.bfloat16), halo], axis=1)
    back = lax.all_to_all(second, "ctx", split_axis=0, concat_axis=0, tiled=True)
    enter_here = back[:, :HEAD_DIM].reshape(GROUPS, HEADS // GROUPS, HEAD_DIM, STATE)
    halo_kv = back[:, HEAD_DIM:].reshape(devices * HALO * share, kv_cols)
    halo_pos = (
        (my_block - HALO + jnp.arange(HALO))[None, :, None] * tok_rows
        + share * jnp.arange(devices)[:, None, None]
        + jnp.arange(share)[None, None, :]
    ).reshape(-1)

    reach = jnp.where((my_seg == my_prev)[:, None], jnp.exp(cum_log), 0.0)
    read_out = jnp.einsum(
        "tgs,gkps->tgkp", readout, enter_here, preferred_element_type=jnp.float32
    ).reshape(tok_rows, HEADS, HEAD_DIM)
    outputs = local_out + read_out * reach[..., None] + skip_gain[0][:, None] * values
    mamba_out = outputs.astype(jnp.bfloat16).reshape(tok_rows, HEADS * HEAD_DIM)
    residual = inputs.astype(jnp.float32) + group_norm(mamba_out.astype(jnp.float32), mamba_gain[0])
    hidden = residual.astype(jnp.bfloat16)

    repeat = QHEADS // KVHEADS
    all_kv = jnp.concatenate([halo_kv, kv], axis=0).reshape(-1, 2, KVHEADS, QDIM)
    keys = all_kv[:, 0]
    vals = all_kv[:, 1]
    key_pos = jnp.concatenate(
        [halo_pos, my_block * tok_rows + jnp.arange(tok_rows, dtype=jnp.int32)]
    )
    key_seg = jnp.take(segment, jnp.maximum(key_pos, 0))
    score_scale = 1.0 / math.sqrt(QDIM)
    pieces = 2
    rows = tok_rows // pieces
    handed = []
    for piece in range(pieces):
        part = slice(piece * rows, (piece + 1) * rows)
        hidden_part = hidden[part]
        if handed:
            hidden_part, _ = lax.optimization_barrier((hidden_part, result))
        queries = hidden_part.reshape(rows, KVHEADS, repeat, QDIM)
        query_pos = my_block * tok_rows + piece * rows + jnp.arange(rows, dtype=jnp.int32)
        allowed = (
            (my_seg[part][:, None] == key_seg[None, :])
            & (key_pos[None, :] <= query_pos[:, None])
            & (key_pos[None, :] >= 0)
        )
        logits = (
            jnp.einsum("tgrd,kgd->grtk", queries, keys, preferred_element_type=jnp.float32)
            * score_scale
        )
        logits = jnp.where(allowed, logits, -1e30)
        best = jnp.max(logits, axis=-1, keepdims=True)
        weights = jnp.exp(logits - best)
        total_weight = jnp.sum(weights, axis=-1)
        blended = jnp.einsum(
            "grtk,kgd->grtd", weights.astype(jnp.bfloat16), vals, preferred_element_type=jnp.float32
        )
        attended = (
            (blended / total_weight[..., None]).transpose(2, 0, 1, 3).reshape(rows, QHEADS * QDIM)
        )
        normed = (
            attended
            * lax.rsqrt(jnp.mean(attended * attended, axis=-1, keepdims=True) + epsilon)
            * attn_gain[0]
        )
        result = (hidden_part.astype(jnp.float32) + normed).astype(jnp.bfloat16)
        handed.append(passed_along(result[None], "phase", 1))
    return jnp.concatenate(handed, axis=1)


def solution(mesh):
    in_specs = (
        P("phase", "ctx", None),
        P("phase", "ctx", None),
        P("phase", "ctx", None),
        P("phase", None),
        P("phase", None),
        P("phase", None),
        P("phase", None),
        P("phase", "ctx", None),
        P("phase", None),
        P("phase", None),
        P(),
    )
    out_specs = P("phase", "ctx", None)
    return jax.shard_map(
        on_device, mesh=mesh, in_specs=in_specs, out_specs=out_specs, check_vma=False
    )
```

```python
import math

import jax
import jax.numpy as jnp
from jax import lax
from jax.experimental import pallas as pl
from jax.experimental.pallas import tpu as pltpu
from jax.sharding import PartitionSpec as P

HEADS = 64
HEAD_DIM = 64
GROUPS = 8
STATE = 128
QHEADS = 32
KVHEADS = 2
QDIM = 128
HALO = 4


precise = lax.Precision.HIGHEST
epsilon = 1e-05


def passed_along(value, axis, steps):
    count = lax.axis_size(axis)
    pairs = [(source, (source + steps) % count) for source in range(count)]
    return lax.ppermute(value, axis, pairs)


def group_norm(values, gain):
    grouped = values.reshape(values.shape[0], GROUPS, -1)
    normed = grouped * lax.rsqrt(jnp.mean(grouped * grouped, axis=-1, keepdims=True) + epsilon)
    return normed.reshape(values.shape) * gain


def block_terms(values, inject, readout, step_sizes, cum_log, seg):
    length = values.shape[0]
    within = HEADS // GROUPS
    positions = jnp.arange(length)
    allowed = (positions[:, None] >= positions[None, :]) & (seg[:, None] == seg[None, :])
    spread = cum_log.T[:, :, None] - cum_log.T[:, None, :]
    decays = jnp.where(allowed[None], jnp.exp(jnp.minimum(spread, 0.0)), 0.0)
    scores = jnp.einsum("tgs,ugs->gtu", readout, inject, preferred_element_type=jnp.float32)
    weights = decays.reshape(GROUPS, within, length, length) * scores[:, None]
    scaled = values * step_sizes[..., None]
    local_out = jnp.einsum(
        "gktu,ugkp->tgkp",
        weights,
        scaled.reshape(length, GROUPS, within, HEAD_DIM),
        precision=precise,
    ).reshape(values.shape)
    ending = cum_log[-1]
    to_end = jnp.where((seg == seg[-1])[:, None], jnp.exp(ending[None, :] - cum_log), 0.0)
    weighted = (scaled * to_end[..., None]).reshape(length, GROUPS, within, HEAD_DIM)
    states = jnp.einsum(
        "tgkp,tgs->gkps", weighted, inject.astype(jnp.float32), precision=precise
    ).reshape(HEADS, HEAD_DIM, STATE)
    return local_out, states, cum_log, ending


def states_kernel(x_ref, bc_ref, raw_ref, bias_ref, rate_ref, seg_ref, tail_ref, out_ref, cum_ref):
    length = raw_ref.shape[0]
    within = HEADS // GROUPS
    shifted = raw_ref[...].astype(jnp.float32) + bias_ref[...]
    steps = jnp.maximum(shifted, 0.0) + jnp.log1p(jnp.exp(-jnp.abs(shifted)))
    cum = -rate_ref[...] * steps
    row = lax.broadcasted_iota(jnp.int32, cum.shape, 0)
    reach = 1
    while reach < length:
        cum = cum + jnp.where(row >= reach, pltpu.roll(cum, reach, 0), 0.0)
        reach *= 2
    cum_ref[...] = cum
    ending = cum[length - 1 : length, :]
    seg = seg_ref[...]
    same = seg == seg[length - 1 : length, :]
    weights = jnp.where(same, jnp.exp(ending - cum), 0.0) * steps
    w_high = weights.astype(jnp.bfloat16)
    w_low = (weights - w_high.astype(jnp.float32)).astype(jnp.bfloat16)
    width = within * HEAD_DIM
    head_of = lax.broadcasted_iota(jnp.int32, (HEADS, width), 0)
    column = lax.broadcasted_iota(jnp.int32, (HEADS, width), 1)
    for group in range(GROUPS):
        spread = (column // HEAD_DIM + group * within == head_of).astype(jnp.bfloat16)
        w = jnp.dot(w_high, spread, preferred_element_type=jnp.float32) + jnp.dot(
            w_low, spread, preferred_element_type=jnp.float32
        )
        scaled = x_ref[:, group * width : (group + 1) * width].astype(jnp.float32) * w
        high = scaled.astype(jnp.bfloat16)
        low = (scaled - high.astype(jnp.float32)).astype(jnp.bfloat16)
        inject = bc_ref[:, group * 2 * STATE : group * 2 * STATE + STATE]
        over_tokens = (((0,), (0,)), ((), ()))
        state = lax.dot_general(
            high, inject, over_tokens, preferred_element_type=jnp.float32
        ) + lax.dot_general(low, inject, over_tokens, preferred_element_type=jnp.float32)
        out_ref[group * within : (group + 1) * within, :HEAD_DIM, :] = (
            state.astype(out_ref.dtype).reshape(within, HEAD_DIM, STATE)
        )
    out_ref[:, HEAD_DIM:, :] = tail_ref[...]


def block_states(inputs, projections, raw, bias, rate, seg, tail):
    tokens = inputs.shape[0]
    rows = HEAD_DIM + tail.shape[1]
    return pl.pallas_call(
        states_kernel,
        out_shape=(
            jax.ShapeDtypeStruct((HEADS, rows, STATE), jnp.bfloat16),
            jax.ShapeDtypeStruct((tokens, HEADS), jnp.float32),
        ),
        cost_estimate=pl.CostEstimate(
            flops=4 * HEADS * HEAD_DIM * STATE * tokens,
            transcendentals=3 * HEADS * tokens,
            bytes_accessed=inputs.size * 2 + projections.size * 2 + HEADS * rows * STATE * 2,
        ),
    )(
        inputs,
        projections,
        raw,
        bias.reshape(1, HEADS),
        rate.reshape(1, HEADS),
        seg.reshape(tokens, 1),
        tail,
    )


def on_device(
    mixer_input,
    state_proj,
    dt_raw,
    decay_rate,
    dt_bias,
    skip_gain,
    mamba_gain,
    keys_values,
    attn_gain,
    documents,
    placement_perm,
):
    devices = lax.axis_size("ctx")
    myself = lax.axis_index("ctx")
    tok_rows = mixer_input.shape[1]
    kv_cols = keys_values.shape[2]
    slice_cols = kv_cols // devices
    inverse = (
        jnp.zeros((devices,), jnp.int32)
        .at[placement_perm]
        .set(jnp.arange(devices, dtype=jnp.int32))
    )
    segment = documents[0]
    block_seg = segment.reshape(devices, tok_rows)
    seg_end = block_seg[:, -1]
    seg_prev = jnp.concatenate([jnp.full((1,), -1, jnp.int32), seg_end[:-1]])
    my_block = placement_perm[myself]
    my_seg = lax.dynamic_slice_in_dim(segment, my_block * tok_rows, tok_rows, 0)
    my_prev = seg_prev[my_block]

    inputs = mixer_input[0]
    values = inputs.astype(jnp.float32).reshape(tok_rows, HEADS, HEAD_DIM)
    paired = state_proj[0].reshape(tok_rows, GROUPS, 2, STATE)
    inject = paired[:, :, 0]
    readout = paired[:, :, 1]
    step_sizes = jax.nn.softplus(dt_raw[0].astype(jnp.float32) + dt_bias[0])
    kv = keys_values[0]
    lanes = 128
    share = tok_rows // devices
    kv_rows = share * kv_cols // lanes
    kv_slices = kv.reshape(devices, kv_rows, lanes)
    raw_cols = dt_raw[0].T.reshape(HEADS, 1, tok_rows)
    used = kv_rows + 1
    padding = jnp.zeros((devices, -used % 8, lanes), jnp.bfloat16)
    tail = jnp.concatenate([kv_slices, raw_cols, padding], axis=1)
    first, cum_log = block_states(
        inputs, state_proj[0], dt_raw[0], dt_bias[0], decay_rate[0], my_seg, tail
    )
    local_out = block_terms(values, inject, readout, step_sizes, cum_log, my_seg)[0]
    got = lax.all_to_all(first, "ctx", split_axis=0, concat_axis=0, tiled=True)
    got_kv = got[:, HEAD_DIM : HEAD_DIM + kv_rows]
    got_raw = got[:, HEAD_DIM + kv_rows].astype(jnp.float32)

    my_rate = decay_rate[0][myself]
    my_bias = dt_bias[0][myself]
    my_steps = jax.nn.softplus(got_raw + my_bias)
    endings = jnp.cumsum(-my_rate * my_steps, axis=1)[:, -1]
    ending_pos = endings[inverse]
    running = jnp.cumsum(ending_pos)
    before = running - ending_pos
    positions = jnp.arange(devices)
    linked = (positions[None, :] < positions[:, None]) & (seg_end[None, :] == seg_prev[:, None])
    factors = jnp.where(
        linked, jnp.exp(jnp.minimum(before[:, None] - running[None, :], 0.0)), 0.0
    )
    by_device = factors[placement_perm][:, placement_perm]
    flat_states = got[:, :HEAD_DIM].reshape(devices, HEAD_DIM * STATE)
    high = by_device.astype(jnp.bfloat16)
    low = (by_device - high.astype(jnp.float32)).astype(jnp.bfloat16)
    entering = jnp.dot(high, flat_states, preferred_element_type=jnp.float32) + jnp.dot(
        low, flat_states, preferred_element_type=jnp.float32
    )
    entering = entering.reshape(devices, HEAD_DIM, STATE)

    halo_blocks = placement_perm[:, None] - HALO + jnp.arange(HALO)[None, :]
    halo_src = inverse[jnp.clip(halo_blocks, 0, devices - 1)]
    halo = got_kv[halo_src].reshape(devices, HALO * kv_rows, lanes)
    second = jnp.concatenate([entering.astype(jnp.bfloat16), halo], axis=1)
    back = lax.all_to_all(second, "ctx", split_axis=0, concat_axis=0, tiled=True)
    enter_here = back[:, :HEAD_DIM].reshape(GROUPS, HEADS // GROUPS, HEAD_DIM, STATE)
    halo_kv = back[:, HEAD_DIM:].reshape(devices * HALO * share, kv_cols)
    halo_pos = (
        (my_block - HALO + jnp.arange(HALO))[None, :, None] * tok_rows
        + share * jnp.arange(devices)[:, None, None]
        + jnp.arange(share)[None, None, :]
    ).reshape(-1)

    reach = jnp.where((my_seg == my_prev)[:, None], jnp.exp(cum_log), 0.0)
    read_out = jnp.einsum(
        "tgs,gkps->tgkp", readout, enter_here, preferred_element_type=jnp.float32
    ).reshape(tok_rows, HEADS, HEAD_DIM)
    outputs = local_out + read_out * reach[..., None] + skip_gain[0][:, None] * values
    mamba_out = outputs.astype(jnp.bfloat16).reshape(tok_rows, HEADS * HEAD_DIM)
    residual = inputs.astype(jnp.float32) + group_norm(mamba_out.astype(jnp.float32), mamba_gain[0])
    hidden = residual.astype(jnp.bfloat16)

    repeat = QHEADS // KVHEADS
    all_kv = jnp.concatenate([halo_kv, kv], axis=0).reshape(-1, 2, KVHEADS, QDIM)
    keys = all_kv[:, 0]
    vals = all_kv[:, 1]
    key_pos = jnp.concatenate(
        [halo_pos, my_block * tok_rows + jnp.arange(tok_rows, dtype=jnp.int32)]
    )
    key_seg = jnp.take(segment, jnp.maximum(key_pos, 0))
    score_scale = 1.0 / math.sqrt(QDIM)
    pieces = 2
    rows = tok_rows // pieces
    handed = []
    for piece in range(pieces):
        part = slice(piece * rows, (piece + 1) * rows)
        hidden_part = hidden[part]
        if handed:
            hidden_part, _ = lax.optimization_barrier((hidden_part, result))
        queries = hidden_part.reshape(rows, KVHEADS, repeat, QDIM)
        query_pos = my_block * tok_rows + piece * rows + jnp.arange(rows, dtype=jnp.int32)
        allowed = (
            (my_seg[part][:, None] == key_seg[None, :])
            & (key_pos[None, :] <= query_pos[:, None])
            & (key_pos[None, :] >= 0)
        )
        logits = (
            jnp.einsum("tgrd,kgd->grtk", queries, keys, preferred_element_type=jnp.float32)
            * score_scale
        )
        logits = jnp.where(allowed, logits, -1e30)
        best = jnp.max(logits, axis=-1, keepdims=True)
        weights = jnp.exp(logits - best)
        total_weight = jnp.sum(weights, axis=-1)
        blended = jnp.einsum(
            "grtk,kgd->grtd", weights.astype(jnp.bfloat16), vals, preferred_element_type=jnp.float32
        )
        attended = (
            (blended / total_weight[..., None]).transpose(2, 0, 1, 3).reshape(rows, QHEADS * QDIM)
        )
        normed = (
            attended
            * lax.rsqrt(jnp.mean(attended * attended, axis=-1, keepdims=True) + epsilon)
            * attn_gain[0]
        )
        result = (hidden_part.astype(jnp.float32) + normed).astype(jnp.bfloat16)
        handed.append(passed_along(result[None], "phase", 1))
    return jnp.concatenate(handed, axis=1)


def solution(mesh):
    in_specs = (
        P("phase", "ctx", None),
        P("phase", "ctx", None),
        P("phase", "ctx", None),
        P("phase", None),
        P("phase", None),
        P("phase", None),
        P("phase", None),
        P("phase", "ctx", None),
        P("phase", None),
        P("phase", None),
        P(),
    )
    out_specs = P("phase", "ctx", None)
    return jax.shard_map(
        on_device, mesh=mesh, in_specs=in_specs, out_specs=out_specs, check_vma=False
    )
```

```python
import math

import jax
import jax.numpy as jnp
from jax import lax
from jax.experimental import pallas as pl
from jax.experimental.pallas import tpu as pltpu
from jax.sharding import PartitionSpec as P

HEADS = 64
HEAD_DIM = 64
GROUPS = 8
STATE = 128
QHEADS = 32
KVHEADS = 2
QDIM = 128
HALO = 4


precise = lax.Precision.HIGHEST
epsilon = 1e-05


def passed_along(value, axis, steps):
    count = lax.axis_size(axis)
    pairs = [(source, (source + steps) % count) for source in range(count)]
    return lax.ppermute(value, axis, pairs)


def group_norm(values, gain):
    grouped = values.reshape(values.shape[0], GROUPS, -1)
    normed = grouped * lax.rsqrt(jnp.mean(grouped * grouped, axis=-1, keepdims=True) + epsilon)
    return normed.reshape(values.shape) * gain


def block_terms(values, inject, readout, step_sizes, rates, seg):
    length = values.shape[0]
    within = HEADS // GROUPS
    cum_log = jnp.cumsum(-rates * step_sizes, axis=0)
    positions = jnp.arange(length)
    allowed = (positions[:, None] >= positions[None, :]) & (seg[:, None] == seg[None, :])
    spread = cum_log.T[:, :, None] - cum_log.T[:, None, :]
    decays = jnp.where(allowed[None], jnp.exp(jnp.minimum(spread, 0.0)), 0.0)
    scores = jnp.einsum("tgs,ugs->gtu", readout, inject, preferred_element_type=jnp.float32)
    weights = decays.reshape(GROUPS, within, length, length) * scores[:, None]
    scaled = values * step_sizes[..., None]
    local_out = jnp.einsum(
        "gktu,ugkp->tgkp",
        weights,
        scaled.reshape(length, GROUPS, within, HEAD_DIM),
        precision=precise,
    ).reshape(values.shape)
    ending = cum_log[-1]
    to_end = jnp.where((seg == seg[-1])[:, None], jnp.exp(ending[None, :] - cum_log), 0.0)
    weighted = (scaled * to_end[..., None]).reshape(length, GROUPS, within, HEAD_DIM)
    states = jnp.einsum(
        "tgkp,tgs->gkps", weighted, inject.astype(jnp.float32), precision=precise
    ).reshape(HEADS, HEAD_DIM, STATE)
    return local_out, states, cum_log, ending


def states_kernel(x_ref, bc_ref, raw_ref, bias_ref, rate_ref, seg_ref, tail_ref, out_ref, cum_ref):
    length = raw_ref.shape[0]
    within = HEADS // GROUPS
    shifted = raw_ref[...].astype(jnp.float32) + bias_ref[...]
    steps = jnp.maximum(shifted, 0.0) + jnp.log1p(jnp.exp(-jnp.abs(shifted)))
    cum = -rate_ref[...] * steps
    row = lax.broadcasted_iota(jnp.int32, cum.shape, 0)
    reach = 1
    while reach < length:
        cum = cum + jnp.where(row >= reach, pltpu.roll(cum, reach, 0), 0.0)
        reach *= 2
    cum_ref[...] = cum
    ending = cum[length - 1 : length, :]
    seg = seg_ref[...]
    same = seg == seg[length - 1 : length, :]
    weights = jnp.where(same, jnp.exp(ending - cum), 0.0) * steps
    w_high = weights.astype(jnp.bfloat16)
    w_low = (weights - w_high.astype(jnp.float32)).astype(jnp.bfloat16)
    width = within * HEAD_DIM
    head_of = lax.broadcasted_iota(jnp.int32, (HEADS, width), 0)
    column = lax.broadcasted_iota(jnp.int32, (HEADS, width), 1)
    for group in range(GROUPS):
        spread = (column // HEAD_DIM + group * within == head_of).astype(jnp.bfloat16)
        w = jnp.dot(w_high, spread, preferred_element_type=jnp.float32) + jnp.dot(
            w_low, spread, preferred_element_type=jnp.float32
        )
        scaled = x_ref[:, group * width : (group + 1) * width].astype(jnp.float32) * w
        high = scaled.astype(jnp.bfloat16)
        low = (scaled - high.astype(jnp.float32)).astype(jnp.bfloat16)
        inject = bc_ref[:, group * 2 * STATE : group * 2 * STATE + STATE]
        over_tokens = (((0,), (0,)), ((), ()))
        state = lax.dot_general(
            high, inject, over_tokens, preferred_element_type=jnp.float32
        ) + lax.dot_general(low, inject, over_tokens, preferred_element_type=jnp.float32)
        out_ref[group * within : (group + 1) * within, :HEAD_DIM, :] = (
            state.astype(out_ref.dtype).reshape(within, HEAD_DIM, STATE)
        )
    out_ref[:, HEAD_DIM:, :] = tail_ref[...]


def block_states(inputs, projections, raw, bias, rate, seg, tail):
    tokens = inputs.shape[0]
    rows = HEAD_DIM + tail.shape[1]
    return pl.pallas_call(
        states_kernel,
        out_shape=(
            jax.ShapeDtypeStruct((HEADS, rows, STATE), jnp.bfloat16),
            jax.ShapeDtypeStruct((tokens, HEADS), jnp.float32),
        ),
        cost_estimate=pl.CostEstimate(
            flops=4 * HEADS * HEAD_DIM * STATE * tokens,
            transcendentals=3 * HEADS * tokens,
            bytes_accessed=inputs.size * 2 + projections.size * 2 + HEADS * rows * STATE * 2,
        ),
    )(
        inputs,
        projections,
        raw,
        bias.reshape(1, HEADS),
        rate.reshape(1, HEADS),
        seg.reshape(tokens, 1),
        tail,
    )


def on_device(
    mixer_input,
    state_proj,
    dt_raw,
    decay_rate,
    dt_bias,
    skip_gain,
    mamba_gain,
    keys_values,
    attn_gain,
    documents,
    placement_perm,
):
    devices = lax.axis_size("ctx")
    myself = lax.axis_index("ctx")
    tok_rows = mixer_input.shape[1]
    kv_cols = keys_values.shape[2]
    slice_cols = kv_cols // devices
    inverse = (
        jnp.zeros((devices,), jnp.int32)
        .at[placement_perm]
        .set(jnp.arange(devices, dtype=jnp.int32))
    )
    segment = documents[0]
    block_seg = segment.reshape(devices, tok_rows)
    seg_end = block_seg[:, -1]
    seg_prev = jnp.concatenate([jnp.full((1,), -1, jnp.int32), seg_end[:-1]])
    my_block = placement_perm[myself]
    my_seg = lax.dynamic_slice_in_dim(segment, my_block * tok_rows, tok_rows, 0)
    my_prev = seg_prev[my_block]

    inputs = mixer_input[0]
    values = inputs.astype(jnp.float32).reshape(tok_rows, HEADS, HEAD_DIM)
    paired = state_proj[0].reshape(tok_rows, GROUPS, 2, STATE)
    inject = paired[:, :, 0]
    readout = paired[:, :, 1]
    step_sizes = jax.nn.softplus(dt_raw[0].astype(jnp.float32) + dt_bias[0])
    local_out, states, cum_log, ending = block_terms(
        values, inject, readout, step_sizes, decay_rate[0], my_seg
    )

    kv = keys_values[0]
    lanes = 128
    share = tok_rows // devices
    kv_rows = share * kv_cols // lanes
    kv_slices = kv.reshape(devices, kv_rows, lanes)
    raw_cols = dt_raw[0].T.reshape(HEADS, 1, tok_rows)
    used = kv_rows + 1
    padding = jnp.zeros((devices, -used % 8, lanes), jnp.bfloat16)
    tail = jnp.concatenate([kv_slices, raw_cols, padding], axis=1)
    first, cum_log = block_states(
        inputs, state_proj[0], dt_raw[0], dt_bias[0], decay_rate[0], my_seg, tail
    )
    got = lax.all_to_all(first, "ctx", split_axis=0, concat_axis=0, tiled=True)
    got_kv = got[:, HEAD_DIM : HEAD_DIM + kv_rows]
    got_raw = got[:, HEAD_DIM + kv_rows].astype(jnp.float32)

    my_rate = decay_rate[0][myself]
    my_bias = dt_bias[0][myself]
    my_steps = jax.nn.softplus(got_raw + my_bias)
    endings = jnp.cumsum(-my_rate * my_steps, axis=1)[:, -1]
    ending_pos = endings[inverse]
    running = jnp.cumsum(ending_pos)
    before = running - ending_pos
    at = placement_perm
    linked = (at[None, :] < at[:, None]) & (seg_end[at][None, :] == seg_prev[at][:, None])
    by_device = jnp.where(
        linked, jnp.exp(jnp.minimum(before[at][:, None] - running[at][None, :], 0.0)), 0.0
    )
    flat_states = got[:, :HEAD_DIM].reshape(devices, HEAD_DIM * STATE)
    high = by_device.astype(jnp.bfloat16)
    low = (by_device - high.astype(jnp.float32)).astype(jnp.bfloat16)
    entering = jnp.dot(high, flat_states, preferred_element_type=jnp.float32) + jnp.dot(
        low, flat_states, preferred_element_type=jnp.float32
    )
    entering = entering.reshape(devices, HEAD_DIM, STATE)

    halo_blocks = placement_perm[:, None] - HALO + jnp.arange(HALO)[None, :]
    halo_src = inverse[jnp.clip(halo_blocks, 0, devices - 1)]
    halo = got_kv[halo_src].reshape(devices, HALO * kv_rows, lanes)
    second = jnp.concatenate([entering.astype(jnp.bfloat16), halo], axis=1)
    back = lax.all_to_all(second, "ctx", split_axis=0, concat_axis=0, tiled=True)
    enter_here = back[:, :HEAD_DIM].reshape(GROUPS, HEADS // GROUPS, HEAD_DIM, STATE)
    halo_kv = back[:, HEAD_DIM:].reshape(devices * HALO * share, kv_cols)
    halo_pos = (
        (my_block - HALO + jnp.arange(HALO))[None, :, None] * tok_rows
        + share * jnp.arange(devices)[:, None, None]
        + jnp.arange(share)[None, None, :]
    ).reshape(-1)

    reach = jnp.where((my_seg == my_prev)[:, None], jnp.exp(cum_log), 0.0)
    read_out = jnp.einsum(
        "tgs,gkps->tgkp", readout, enter_here, preferred_element_type=jnp.float32
    ).reshape(tok_rows, HEADS, HEAD_DIM)
    outputs = local_out + read_out * reach[..., None] + skip_gain[0][:, None] * values
    mamba_out = outputs.astype(jnp.bfloat16).reshape(tok_rows, HEADS * HEAD_DIM)
    residual = inputs.astype(jnp.float32) + group_norm(mamba_out.astype(jnp.float32), mamba_gain[0])
    hidden = residual.astype(jnp.bfloat16)

    repeat = QHEADS // KVHEADS
    all_kv = jnp.concatenate([halo_kv, kv], axis=0).reshape(-1, 2, KVHEADS, QDIM)
    keys = all_kv[:, 0]
    vals = all_kv[:, 1]
    key_pos = jnp.concatenate(
        [halo_pos, my_block * tok_rows + jnp.arange(tok_rows, dtype=jnp.int32)]
    )
    key_seg = jnp.take(segment, jnp.maximum(key_pos, 0))
    score_scale = 1.0 / math.sqrt(QDIM)
    pieces = 2
    rows = tok_rows // pieces
    handed = []
    for piece in range(pieces):
        part = slice(piece * rows, (piece + 1) * rows)
        hidden_part = hidden[part]
        if handed:
            hidden_part, _ = lax.optimization_barrier((hidden_part, result))
        queries = hidden_part.reshape(rows, KVHEADS, repeat, QDIM)
        query_pos = my_block * tok_rows + piece * rows + jnp.arange(rows, dtype=jnp.int32)
        allowed = (
            (my_seg[part][:, None] == key_seg[None, :])
            & (key_pos[None, :] <= query_pos[:, None])
            & (key_pos[None, :] >= 0)
        )
        logits = (
            jnp.einsum("tgrd,kgd->grtk", queries, keys, preferred_element_type=jnp.float32)
            * score_scale
        )
        logits = jnp.where(allowed, logits, -1e30)
        best = jnp.max(logits, axis=-1, keepdims=True)
        weights = jnp.exp(logits - best)
        total_weight = jnp.sum(weights, axis=-1)
        blended = jnp.einsum(
            "grtk,kgd->grtd", weights.astype(jnp.bfloat16), vals, preferred_element_type=jnp.float32
        )
        attended = (
            (blended / total_weight[..., None]).transpose(2, 0, 1, 3).reshape(rows, QHEADS * QDIM)
        )
        normed = (
            attended
            * lax.rsqrt(jnp.mean(attended * attended, axis=-1, keepdims=True) + epsilon)
            * attn_gain[0]
        )
        result = (hidden_part.astype(jnp.float32) + normed).astype(jnp.bfloat16)
        handed.append(passed_along(result[None], "phase", 1))
    return jnp.concatenate(handed, axis=1)


def solution(mesh):
    in_specs = (
        P("phase", "ctx", None),
        P("phase", "ctx", None),
        P("phase", "ctx", None),
        P("phase", None),
        P("phase", None),
        P("phase", None),
        P("phase", None),
        P("phase", "ctx", None),
        P("phase", None),
        P("phase", None),
        P(),
    )
    out_specs = P("phase", "ctx", None)
    return jax.shard_map(
        on_device, mesh=mesh, in_specs=in_specs, out_specs=out_specs, check_vma=False
    )
```
